32 devices in a mesh: seq: 16 (over z, y, core), fsdp: 2 (over x).
Axes of the slice: x: 2, y: 2, z: 4, core: 2. Of those that a mesh axis runs over, the one named last changes fastest.
Arguments:
- queries: bfloat16 [2, 8192, 1024], P('fsdp', 'seq'), may hold values from -10.5 to 10.5
- key_vectors: bfloat16 [2, 8192, 1024], P('fsdp', 'seq'), may hold values from -10.5 to 10.5
- value_vectors: bfloat16 [2, 8192, 1024], P('fsdp', 'seq'), may hold values from -6 to 6
- grad_mixed: bfloat16 [2, 8192, 2048], P('fsdp', 'seq'), may hold values from -24 to 24
- out_weight: bfloat16 [1024, 2048], P('fsdp'), may hold values from -0.1875 to 0.1875
- head_phase: int32 [8], replicated, may hold values from 0 to 3
- segments_short: int32 [7], replicated, may hold values from 1 to 2048, 8192 in all
- segments_long: int32 [1], replicated, may hold values from 1 to 8192, as said below
Outputs:
- grad_query: bfloat16 [2, 8192, 1024], P('fsdp', 'seq')
- grad_key: bfloat16 [2, 8192, 1024], P('fsdp', 'seq')
- grad_value: bfloat16 [2, 8192, 1024], P('fsdp', 'seq')
The draws below stay inside these ranges and needn't reach their ends.
Inputs may be any that keep to these rules, and one draw needn't show every extreme that they name: `segments_long`: lengths that sum to 8192; the last of them is 8192, the others are shorter.
All inputs are finite; a program needn't handle non-finite values.
Results may differ from the reference program's by a relative error of at most 0.0095.
Values may be sent and summed in bfloat16 or wider, within the bound.
No kernel may reach another device: no remote copies, remote signals or barrier semaphores. Data moves between devices by JAX's collectives and lax.ppermute only.
A program may use at most 256 MiB of HBM per device.

```python
import math
import jax
import jax.numpy as jnp
import numpy as np
from jax import lax

D = 2048
HEADS = 8
HS = 128
TOK_DEV = 512
SEG_SHORT = 2048
SEG_LONG = 8192
GROUPS = 2
L = 8192
REACH_SHORT = 4
REACH_LONG = 16
NSEG_SHORT = 7
NSEG_LONG = 1
N_SEQ = 16


def draw_queries(key, part):
    drawn = jnp.clip(jax.random.normal(jax.random.fold_in(key, 21), (GROUPS, L, HEADS * HS), jnp.float32), -6.0, 6.0)
    return drawn.astype(jnp.bfloat16)


def draw_key_vectors(key, part):
    drawn = jnp.clip(jax.random.normal(jax.random.fold_in(key, 22), (GROUPS, L, HEADS * HS), jnp.float32), -6.0, 6.0)
    return drawn.astype(jnp.bfloat16)


def split_lengths(key, total, count):
    base = total // count
    extra = total % count
    places = jnp.arange(count, dtype=jnp.int32)
    pieces = base + (places < extra).astype(jnp.int32)
    if count > 1:
        room = max(min(base - 1, SEG_LONG - base - 2), 0)
        moves = jax.random.randint(key, (count - 1,), 0, room + 1, dtype=jnp.int32)
        zero_one = jnp.zeros((1,), jnp.int32)
        pieces = pieces + jnp.concatenate([moves, zero_one]) - jnp.concatenate([zero_one, moves])
    return pieces.astype(jnp.int32)


def draw_segments_long(key, part):
    if NSEG_LONG == 1:
        return jnp.full((1,), L, jnp.int32)
    before = split_lengths(jax.random.fold_in(key, 32), L - SEG_LONG, NSEG_LONG - 1)
    return jnp.concatenate([before, jnp.full((1,), SEG_LONG, jnp.int32)]).astype(jnp.int32)


def plant(result, own_key, least, high):
    longest = result.shape.index(max(result.shape))
    spots = []
    for shift in (0, 1):
        where = [jax.random.randint(jax.random.fold_in(own_key, axis), (), 0, length) for axis, length in enumerate(result.shape)]
        where[longest] = (where[longest] + shift) % result.shape[longest]
        spots.append(tuple(where))
    return result.at[spots[0]].set(least).at[spots[1]].set(high)


def level_of(stream_key, extent, shards, low, largest):
    loudness, own = 1.0, jax.random.fold_in(stream_key, 6)
    for dim, blocks in shards:
        heights = jnp.exp(jax.random.uniform(jax.random.fold_in(own, dim), (blocks,), jnp.float32, low / len(shards), largest / len(shards)))
        loudness = loudness * jnp.repeat(heights, extent[dim] // blocks).reshape([-1 if axis == dim else 1 for axis in range(len(extent))])
    return loudness


def length_profile(amount, total, most, lean):
    loads = [(1 << 20) // math.isqrt(rank ** lean) + 1 for rank in range(2, amount + 1)]
    rest, given = total - most - (amount - 1), [1] * (amount - 1)
    while rest > 0:
        free = [i for i in range(amount - 1) if given[i] < most]
        mass, budget = sum([loads[i] for i in free]), rest
        for i in free:
            more = min(most - given[i], max(1, budget * loads[i] // mass), rest)
            given[i] = given[i] + more
            rest = rest - more
    return np.array([most] + given)


def ragged_sizes(key, count, total, most, skew):
    if count == 2:
        one = jax.random.randint(key, (), max(1, total - most), min(most, total - 1) + 1)
        return jnp.stack([one, total - one])
    tallies = jnp.asarray(length_profile(count, total, most, skew), jnp.int32)
    twos = (count - 1) // 2
    source_of, sink = tallies[1:1 + 2 * twos:2], tallies[2:2 + 2 * twos:2]
    room = jnp.minimum(source_of - 1, most - sink)
    shifted = jax.random.randint(jax.random.fold_in(key, 1), (twos,), 0, 1 << 20) % (room + 1)
    tallies = tallies.at[1:1 + 2 * twos:2].set(source_of - shifted).at[2:2 + 2 * twos:2].set(sink + shifted)
    return tallies[jax.random.permutation(jax.random.fold_in(key, 2), count)]


def noise(own_key, dims, scale, limit, cuts=(), kind=jnp.bfloat16):
    drawn = scale * jax.random.normal(own_key, dims, jnp.float32)
    if cuts:
        drawn = drawn * level_of(own_key, dims, cuts, -0.22, 0.18)
    return jnp.clip(drawn, -limit, limit).astype(kind)


def setup_inputs(seed: int = 0) -> dict:
    key_list = jax.random.split(jax.random.key(seed), 9)
    queries = draw_queries(jax.random.fold_in(key_list[8], 71), 0)
    key_vectors = draw_key_vectors(jax.random.fold_in(key_list[8], 71), 0)
    value_vectors = noise(key_list[2], (GROUPS, L, HEADS * HS), 1.0, 6.0, ((0, 2), (1, 16)))
    grad_mixed = noise(key_list[3], (GROUPS, L, D), 4.0, 24.0, ((0, 2), (1, 16)))
    out_weight = noise(key_list[4], (HEADS * HS, D), (HEADS * HS) ** -0.5, 0.1875, ((0, 2),))
    head_phase = plant(jax.random.randint(key_list[5], (HEADS,), 0, 4), jax.random.fold_in(key_list[5], 1), 0, 3).astype(jnp.int32)
    segments_short = ragged_sizes(key_list[6], NSEG_SHORT, L, SEG_SHORT, 2).astype(jnp.int32)
    segments_long = draw_segments_long(jax.random.fold_in(key_list[8], 71), 0)
    return dict(queries=queries, key_vectors=key_vectors, value_vectors=value_vectors, grad_mixed=grad_mixed, out_weight=out_weight, head_phase=head_phase, segments_short=segments_short, segments_long=segments_long)


VERY_NEGATIVE = -1e+30

def take_half(tensor, parity):
    layout = tensor.shape
    paired = tensor.reshape(layout[:-3] + (layout[-3] // 2, 2) + layout[-2:])
    return jnp.where((parity == 0)[:, None], paired[..., 0, :, :], paired[..., 1, :, :])

def put_half(tensor, parity):
    zero_fill = jnp.zeros_like(tensor)
    first_half = jnp.where((parity == 0)[:, None], tensor, zero_fill)
    second_half = jnp.where((parity == 1)[:, None], tensor, zero_fill)
    stacked = jnp.stack([first_half, second_half], axis=-3)
    return stacked.reshape(tensor.shape[:-3] + (2 * tensor.shape[-3],) + tensor.shape[-2:])

def stat_half(tensor, parity):
    paired = tensor.reshape(tensor.shape[0], tensor.shape[1] // 2, 2)
    return jnp.where((parity == 0)[:, None], paired[:, :, 0], paired[:, :, 1])

def stat_put(tensor, parity, fill_value):
    filler = jnp.full_like(tensor, fill_value)
    first_half = jnp.where((parity == 0)[:, None], tensor, filler)
    second_half = jnp.where((parity == 1)[:, None], tensor, filler)
    return jnp.stack([first_half, second_half], axis=-1).reshape(tensor.shape[0], 2 * tensor.shape[1])

def segment_of(positions, lengths):
    seg_ends = jnp.cumsum(lengths).astype(jnp.int32)
    return lax.optimization_barrier(jnp.sum((positions[..., None] >= seg_ends).astype(jnp.int32), axis=-1))

def row_positions(shard_index, tok_dev, stride, offset, row_count):
    return shard_index * tok_dev + stride * jnp.arange(row_count, dtype=jnp.int32)[None, :] + offset[:, None]

def pair_mask(query_pos, key_pos, lengths):
    query_seg = segment_of(query_pos, lengths)
    key_seg = segment_of(key_pos, lengths)
    causal = key_pos[:, None, :] <= query_pos[:, :, None]
    same_seg = key_seg[:, None, :] == query_seg[:, :, None]
    return causal & same_seg & (key_pos[:, None, :] >= 0)

def product(pattern, left_operand, right_operand):
    return jnp.einsum(pattern, left_operand.astype(jnp.float32), right_operand.astype(jnp.float32))

def unguarded(is_live, compute, shapes):
    return compute()

def shard_grads(shard_index, query_rows, grad_rows, near_window, far_window, head_phase, segments_short, segments_long, guard_fn, product_fn):
    rows_short, head_count, head_width = query_rows.shape
    tok_dev = 2 * rows_short
    score_scale = 1.0 / math.sqrt(head_width)
    par_short = head_phase % 2
    par_long = head_phase // 2
    query_long = take_half(query_rows, par_long)
    grad_long = take_half(grad_rows, par_long)
    levels = [(query_rows, grad_rows, near_window, 2, par_short, segments_short), (query_long, grad_long, far_window, 4, head_phase, segments_long)]
    stored = []
    peak_list = []
    for query_here, grad_here, window, stride, offset, lengths in levels:
        row_count = query_here.shape[0]
        query_pos = row_positions(shard_index, tok_dev, stride, offset, row_count)
        blocks = []
        top_here = jnp.full((head_count, row_count), VERY_NEGATIVE, jnp.float32)
        for distance in range(len(window)):
            key_pos = row_positions(shard_index - distance, tok_dev, stride, offset, row_count)
            live_pairs = pair_mask(query_pos, key_pos, lengths)

            def score_block(query_here=query_here, key_here=window[distance][0]):
                return (product_fn('qhd,khd->hqk', query_here, key_here) * score_scale,)
            raw_scores = guard_fn(jnp.any(live_pairs), score_block, ((head_count, row_count, row_count),))[0]
            scores = jnp.where(live_pairs, raw_scores, VERY_NEGATIVE)
            top_here = jnp.maximum(top_here, lax.optimization_barrier(jnp.max(scores, axis=-1)))
            blocks.append((live_pairs, scores))
        stored.append(blocks)
        peak_list.append(top_here)
    top_short = jnp.maximum(peak_list[0], stat_put(peak_list[1], par_long, VERY_NEGATIVE))
    level_tops = [top_short, stat_half(top_short, par_long)]
    totals = []
    numerators = []
    for level_index, (query_here, grad_here, window, stride, offset, lengths) in enumerate(levels):
        row_count = query_here.shape[0]
        total_here = jnp.zeros((head_count, row_count), jnp.float32)
        numer_here = jnp.zeros((row_count, head_count, head_width), jnp.float32)
        for distance, (live_pairs, scores) in enumerate(stored[level_index]):
            weights = jnp.where(live_pairs, jnp.exp(scores - level_tops[level_index][:, :, None]), 0.0)
            total_here = total_here + lax.optimization_barrier(jnp.sum(weights, axis=-1))

            def weight_block(weights=weights, value_here=window[distance][1]):
                return (product_fn('hqk,khd->qhd', weights.astype(jnp.bfloat16), value_here),)
            numer_here = numer_here + guard_fn(jnp.any(live_pairs), weight_block, ((row_count, head_count, head_width),))[0]
        totals.append(total_here)
        numerators.append(numer_here)
    denominator = totals[0] + stat_put(totals[1], par_long, 0.0)
    attended = (numerators[0] + put_half(numerators[1], par_long)) / jnp.transpose(denominator)[:, :, None]
    delta_rows = jnp.transpose(lax.optimization_barrier(jnp.sum(grad_rows.astype(jnp.float32) * attended, axis=-1)))
    inverse = 1.0 / denominator
    level_inverse = [inverse, stat_half(inverse, par_long)]
    level_delta = [delta_rows, stat_half(delta_rows, par_long)]
    grad_levels = []
    part_levels = []
    for level_index, (query_here, grad_here, window, stride, offset, lengths) in enumerate(levels):
        row_count = query_here.shape[0]
        grad_sum = jnp.zeros((row_count, head_count, head_width), jnp.float32)
        part_list = []
        for distance, (live_pairs, scores) in enumerate(stored[level_index]):

            def backward_block(live_pairs=live_pairs, scores=scores, key_here=window[distance][0], value_here=window[distance][1], query_here=query_here, grad_here=grad_here, top_here=level_tops[level_index], inverse_here=level_inverse[level_index], delta_here=level_delta[level_index]):
                probability = jnp.where(live_pairs, jnp.exp(scores - top_here[:, :, None]), 0.0) * inverse_here[:, :, None]
                grad_probs = product_fn('qhd,khd->hqk', grad_here, value_here)
                grad_scores = (probability * (grad_probs - delta_here[:, :, None])).astype(jnp.bfloat16)
                return (product_fn('hqk,khd->qhd', grad_scores, key_here) * score_scale, product_fn('hqk,qhd->khd', grad_scores, query_here) * score_scale, product_fn('hqk,qhd->khd', probability.astype(jnp.bfloat16), grad_here))
            shapes = ((row_count, head_count, head_width),) * 3
            add_query, part_key, part_value = guard_fn(jnp.any(live_pairs), backward_block, shapes)
            grad_sum = grad_sum + add_query
            part_list.append((part_key, part_value))
        grad_levels.append(grad_sum)
        part_levels.append(part_list)
    grad_query = grad_levels[0] + put_half(grad_levels[1], par_long)
    near_parts = []
    for distance in range(len(near_window)):
        key_part = part_levels[0][distance][0] + put_half(part_levels[1][distance][0], par_long)
        value_part = part_levels[0][distance][1] + put_half(part_levels[1][distance][1], par_long)
        near_parts.append(jnp.stack([key_part, value_part]).astype(jnp.bfloat16))
    far_parts = [jnp.stack([part_levels[1][distance][0], part_levels[1][distance][1]]).astype(jnp.bfloat16) for distance in range(len(near_window), len(far_window))]
    return (grad_query, near_parts, far_parts)

def one_sequence(queries, key_vectors, value_vectors, grad_out, head_phase, segments_short, segments_long):
    par_short = head_phase % 2
    par_long = head_phase // 2
    rows_short = TOK_DEV // 2
    rows_long = TOK_DEV // 4
    query_all = take_half(queries.reshape(L, HEADS, HS), par_short)
    grad_all = take_half(grad_out.reshape(L, HEADS, HS), par_short)
    pair_short = jnp.stack([take_half(key_vectors.reshape(L, HEADS, HS), par_short), take_half(value_vectors.reshape(L, HEADS, HS), par_short)])
    pair_long = take_half(pair_short, par_long)
    padded_short = jnp.pad(pair_short, ((0, 0), (REACH_LONG * rows_short, 0), (0, 0), (0, 0)))
    padded_long = jnp.pad(pair_long, ((0, 0), (REACH_LONG * rows_long, 0), (0, 0), (0, 0)))

    def per_shard(accumulated, shard_index):
        query_rows = lax.dynamic_slice_in_dim(query_all, shard_index * rows_short, rows_short, 0)
        grad_rows = lax.dynamic_slice_in_dim(grad_all, shard_index * rows_short, rows_short, 0)
        near_window = [lax.dynamic_slice_in_dim(padded_short, (shard_index - distance + REACH_LONG) * rows_short, rows_short, 1) for distance in range(REACH_SHORT + 1)]
        far_window = [lax.dynamic_slice_in_dim(padded_long, (shard_index - distance + REACH_LONG) * rows_long, rows_long, 1) for distance in range(REACH_LONG + 1)]
        grad_query, near_parts, far_parts = shard_grads(shard_index, query_rows, grad_rows, near_window, far_window, head_phase, segments_short, segments_long, unguarded, product)
        for distance in range(REACH_SHORT + 1):
            place_at = (shard_index - distance + REACH_LONG) * rows_short
            current = lax.dynamic_slice_in_dim(accumulated, place_at, rows_short, 1)
            accumulated = lax.dynamic_update_slice_in_dim(accumulated, current + near_parts[distance].astype(jnp.float32), place_at, 1)
        for distance in range(REACH_SHORT + 1, REACH_LONG + 1):
            place_at = (shard_index - distance + REACH_LONG) * rows_short
            current = lax.dynamic_slice_in_dim(accumulated, place_at, rows_short, 1)
            spread = put_half(far_parts[distance - REACH_SHORT - 1].astype(jnp.float32), par_long)
            accumulated = lax.dynamic_update_slice_in_dim(accumulated, current + spread, place_at, 1)
        return (accumulated, grad_query)
    accumulated = jnp.zeros((2, (N_SEQ + REACH_LONG) * rows_short, HEADS, HS), jnp.float32)
    accumulated, grad_queries = lax.scan(per_shard, accumulated, jnp.arange(N_SEQ, dtype=jnp.int32))
    grad_query_rows = grad_queries.reshape(L // 2, HEADS, HS).astype(jnp.bfloat16)
    final_pair = accumulated[:, REACH_LONG * rows_short:].astype(jnp.bfloat16)
    grad_query = put_half(grad_query_rows, par_short).reshape(L, HEADS * HS)
    grad_key = put_half(final_pair[0], par_short).reshape(L, HEADS * HS)
    grad_value = put_half(final_pair[1], par_short).reshape(L, HEADS * HS)
    return (grad_query, grad_key, grad_value)

def reference(queries, key_vectors, value_vectors, grad_mixed, out_weight, head_phase, segments_short, segments_long):

    def per_sequence(seq_index):
        grad_out = jnp.dot(grad_mixed[seq_index], jnp.transpose(out_weight), preferred_element_type=jnp.float32).astype(jnp.bfloat16)
        return one_sequence(queries[seq_index], key_vectors[seq_index], value_vectors[seq_index], grad_out, head_phase, segments_short, segments_long)
    results = lax.map(per_sequence, jnp.arange(GROUPS, dtype=jnp.int32))
    return (results[0], results[1], results[2])
```

```python
import math

import jax
import jax.numpy as jnp
from jax import lax
from jax.sharding import PartitionSpec as P

REACH_SHORT = 4
REACH_LONG = 16


VERY_NEGATIVE = -1e30


def passed_along(value, axis, by):
    devices = lax.axis_size(axis)
    pairs = [(i, i + by) for i in range(devices) if 0 <= i + by < devices]
    return lax.ppermute(value, axis, pairs)


def take_half(tensor, parity):
    layout = tensor.shape
    paired = tensor.reshape(layout[:-3] + (layout[-3] // 2, 2) + layout[-2:])
    return jnp.where((parity == 0)[:, None], paired[..., 0, :, :], paired[..., 1, :, :])


def put_half(tensor, parity):
    zero_fill = jnp.zeros_like(tensor)
    first_half = jnp.where((parity == 0)[:, None], tensor, zero_fill)
    second_half = jnp.where((parity == 1)[:, None], tensor, zero_fill)
    stacked = jnp.stack([first_half, second_half], axis=-3)
    return stacked.reshape(tensor.shape[:-3] + (2 * tensor.shape[-3],) + tensor.shape[-2:])


def stat_half(tensor, parity):
    paired = tensor.reshape(tensor.shape[:-1] + (tensor.shape[-1] // 2, 2))
    return jnp.where((parity == 0)[:, None], paired[..., 0], paired[..., 1])


def stat_put(tensor, parity, fill_value):
    filler = jnp.full_like(tensor, fill_value)
    first_half = jnp.where((parity == 0)[:, None], tensor, filler)
    second_half = jnp.where((parity == 1)[:, None], tensor, filler)
    return jnp.stack([first_half, second_half], axis=-1).reshape(
        tensor.shape[:-1] + (2 * tensor.shape[-1],)
    )


def segment_of(positions, lengths):
    seg_ends = jnp.cumsum(lengths)
    return jnp.sum((positions[..., None] >= seg_ends).astype(jnp.int32), axis=-1)


def row_positions(shard_index, tok_dev, stride, offset, row_count):
    return (
        shard_index * tok_dev
        + stride * jnp.arange(row_count, dtype=jnp.int32)[None, :]
        + offset[:, None]
    )


def window_positions(shard_index, distances, tok_dev, stride, offset, row_count):
    return jnp.concatenate(
        [row_positions(shard_index + d, tok_dev, stride, offset, row_count) for d in distances],
        axis=1,
    )


def pair_mask(query_pos, key_pos, lengths, total):
    query_seg = segment_of(query_pos, lengths)
    key_seg = segment_of(key_pos, lengths)
    causal = key_pos[:, None, :] <= query_pos[:, :, None]
    same_seg = key_seg[:, None, :] == query_seg[:, :, None]
    valid = (key_pos[:, None, :] >= 0) & (query_pos[:, :, None] < total)
    return causal & same_seg & valid


def product(pattern, left_operand, right_operand):
    return jnp.einsum(pattern, left_operand, right_operand, preferred_element_type=jnp.float32)


def query_side(shard_index, total, q_rows, g_rows, near_kv, far_kv, head_phase, seg_short, seg_long):
    rows_short, head_count, head_width = q_rows.shape
    tok_dev = 2 * rows_short
    scale = 1.0 / math.sqrt(head_width)
    par_short = head_phase % 2
    par_long = head_phase // 2
    levels = [
        (q_rows, g_rows, near_kv, 2, par_short, seg_short),
        (take_half(q_rows, par_long), take_half(g_rows, par_long), far_kv, 4, head_phase, seg_long),
    ]
    stored = []
    peaks = []
    for query_here, grad_here, window, stride, offset, lengths in levels:
        row_count = query_here.shape[0]
        keys = jnp.concatenate([w[0] for w in window], axis=0)
        values = jnp.concatenate([w[1] for w in window], axis=0)
        query_pos = row_positions(shard_index, tok_dev, stride, offset, row_count)
        key_pos = window_positions(
            shard_index, [-d for d in range(len(window))], tok_dev, stride, offset, row_count
        )
        live = pair_mask(query_pos, key_pos, lengths, total)
        scores = jnp.where(live, product("qhd,khd->hqk", query_here, keys) * scale, VERY_NEGATIVE)
        peaks.append(jnp.max(scores, axis=-1))
        stored.append((live, scores, keys, values))
    top_short = jnp.maximum(peaks[0], stat_put(peaks[1], par_long, VERY_NEGATIVE))
    level_tops = [top_short, stat_half(top_short, par_long)]
    totals = []
    numerators = []
    for level_index, (live, scores, keys, values) in enumerate(stored):
        weights = jnp.where(live, jnp.exp(scores - level_tops[level_index][:, :, None]), 0.0)
        totals.append(jnp.sum(weights, axis=-1))
        numerators.append(product("hqk,khd->qhd", weights.astype(jnp.bfloat16), values))
    denominator = totals[0] + stat_put(totals[1], par_long, 0.0)
    attended = (numerators[0] + put_half(numerators[1], par_long)) / jnp.transpose(denominator)[
        :, :, None
    ]
    delta_rows = jnp.transpose(jnp.sum(g_rows.astype(jnp.float32) * attended, axis=-1))
    inverse = 1.0 / denominator
    level_inverse = [inverse, stat_half(inverse, par_long)]
    level_delta = [delta_rows, stat_half(delta_rows, par_long)]
    grads = []
    for level_index, (live, scores, keys, values) in enumerate(stored):
        grad_here = levels[level_index][1]
        probability = (
            jnp.where(live, jnp.exp(scores - level_tops[level_index][:, :, None]), 0.0)
            * level_inverse[level_index][:, :, None]
        )
        grad_probs = product("qhd,khd->hqk", grad_here, values)
        grad_scores = (probability * (grad_probs - level_delta[level_index][:, :, None])).astype(
            jnp.bfloat16
        )
        grads.append(product("hqk,khd->qhd", grad_scores, keys) * scale)
    grad_query = grads[0] + put_half(grads[1], par_long)
    return grad_query, jnp.stack([top_short, inverse, delta_rows])


def key_side(shard_index, total, k_rows, v_rows, near_qg, near_stats, far_qg, far_stats, head_phase, seg_short, seg_long):
    rows_short, head_count, head_width = k_rows.shape
    tok_dev = 2 * rows_short
    scale = 1.0 / math.sqrt(head_width)
    par_short = head_phase % 2
    par_long = head_phase // 2
    levels = [
        (k_rows, v_rows, near_qg, near_stats, 2, par_short, seg_short),
        (take_half(k_rows, par_long), take_half(v_rows, par_long), far_qg, far_stats, 4, head_phase, seg_long),
    ]
    results = []
    for key_here, value_here, window, stats, stride, offset, lengths in levels:
        row_count = key_here.shape[0]
        queries = jnp.concatenate([w[0] for w in window], axis=0)
        grads = jnp.concatenate([w[1] for w in window], axis=0)
        row_stats = jnp.concatenate(stats, axis=-1)
        key_pos = row_positions(shard_index, tok_dev, stride, offset, row_count)
        query_pos = window_positions(
            shard_index, list(range(len(window))), tok_dev, stride, offset, row_count
        )
        live = pair_mask(query_pos, key_pos, lengths, total)
        scores = jnp.where(live, product("qhd,khd->hqk", queries, key_here) * scale, VERY_NEGATIVE)
        probability = (
            jnp.where(live, jnp.exp(scores - row_stats[0][:, :, None]), 0.0)
            * row_stats[1][:, :, None]
        )
        grad_probs = product("qhd,khd->hqk", grads, value_here)
        grad_scores = (probability * (grad_probs - row_stats[2][:, :, None])).astype(jnp.bfloat16)
        grad_key = product("hqk,qhd->khd", grad_scores, queries) * scale
        grad_value = product("hqk,qhd->khd", probability.astype(jnp.bfloat16), grads)
        results.append((grad_key, grad_value))
    grad_key = results[0][0] + put_half(results[1][0], par_long)
    grad_value = results[0][1] + put_half(results[1][1], par_long)
    return grad_key, grad_value


def shards(
    queries,
    key_vectors,
    value_vectors,
    grad_mixed,
    out_weight,
    head_phase,
    segments_short,
    segments_long,
):
    shard_index = lax.axis_index("seq")
    devices = lax.axis_size("seq")
    tok_dev = queries.shape[1]
    total = devices * tok_dev
    head_count = head_phase.shape[0]
    head_width = queries.shape[2] // head_count
    par_short = head_phase % 2
    par_long = head_phase // 2

    def split_rows(tensor):
        return take_half(tensor.reshape(tok_dev, head_count, head_width), par_short)

    near_steps = [d for d in range(1, REACH_SHORT + 1) if d < devices]
    far_steps = [d for d in range(REACH_SHORT + 1, REACH_LONG + 1) if d < devices]

    own_kv = jnp.stack([split_rows(key_vectors[0]), split_rows(value_vectors[0])])
    own_kv_long = take_half(own_kv, par_long)
    near_kv = [own_kv] + [passed_along(own_kv, "seq", d) for d in near_steps]
    far_kv = [take_half(w, par_long) for w in near_kv] + [
        passed_along(own_kv_long, "seq", d) for d in far_steps
    ]

    q_rows = split_rows(queries[0])
    grad_out = jnp.einsum(
        "td,rd->tr",
        grad_mixed[0],
        lax.all_gather(out_weight, "fsdp", axis=0, tiled=True),
        preferred_element_type=jnp.float32,
    ).astype(jnp.bfloat16)
    g_rows = split_rows(grad_out)
    own_qg = jnp.stack([q_rows, g_rows])
    own_qg_long = take_half(own_qg, par_long)
    near_qg = [own_qg] + [passed_along(own_qg, "seq", -d) for d in near_steps]
    far_qg = [take_half(w, par_long) for w in near_qg] + [
        passed_along(own_qg_long, "seq", -d) for d in far_steps
    ]

    grad_query, own_stats = query_side(
        shard_index, total, q_rows, g_rows, near_kv, far_kv, head_phase, segments_short, segments_long
    )
    own_stats_long = stat_half(own_stats, par_long)
    near_stats = [own_stats] + [passed_along(own_stats, "seq", -d) for d in near_steps]
    far_stats = [stat_half(s, par_long) for s in near_stats] + [
        passed_along(own_stats_long, "seq", -d) for d in far_steps
    ]
    grad_key, grad_value = key_side(
        shard_index,
        total,
        own_kv[0],
        own_kv[1],
        near_qg,
        near_stats,
        far_qg,
        far_stats,
        head_phase,
        segments_short,
        segments_long,
    )

    def to_tokens(rows_here):
        return put_half(rows_here, par_short).reshape(1, tok_dev, head_count * head_width)

    return (
        to_tokens(grad_query.astype(jnp.bfloat16)),
        to_tokens(grad_key.astype(jnp.bfloat16)),
        to_tokens(grad_value.astype(jnp.bfloat16)),
    )


def solution(mesh):
    placed = (
        P("fsdp", "seq", None),
        P("fsdp", "seq", None),
        P("fsdp", "seq", None),
        P("fsdp", "seq", None),
        P("fsdp", None),
        P(),
        P(),
        P(),
    )
    return jax.shard_map(
        shards,
        mesh=mesh,
        in_specs=placed,
        out_specs=(P("fsdp", "seq", None), P("fsdp", "seq", None), P("fsdp", "seq", None)),
        check_vma=False,
    )
```

```python
import math

import jax
import jax.numpy as jnp
from jax import lax
from jax.sharding import PartitionSpec as P

REACH_SHORT = 4
REACH_LONG = 16


VERY_NEGATIVE = -1e30


def passed_along(value, axis, by):
    devices = lax.axis_size(axis)
    pairs = [(i, i + by) for i in range(devices) if 0 <= i + by < devices]
    return lax.ppermute(value, axis, pairs)


def take_half(tensor, parity):
    layout = tensor.shape
    paired = tensor.reshape(layout[:-3] + (layout[-3] // 2, 2) + layout[-2:])
    return jnp.where((parity == 0)[:, None], paired[..., 0, :, :], paired[..., 1, :, :])


def put_half(tensor, parity):
    zero_fill = jnp.zeros_like(tensor)
    first_half = jnp.where((parity == 0)[:, None], tensor, zero_fill)
    second_half = jnp.where((parity == 1)[:, None], tensor, zero_fill)
    stacked = jnp.stack([first_half, second_half], axis=-3)
    return stacked.reshape(tensor.shape[:-3] + (2 * tensor.shape[-3],) + tensor.shape[-2:])


def stat_half(tensor, parity):
    paired = tensor.reshape(tensor.shape[:-1] + (tensor.shape[-1] // 2, 2))
    return jnp.where((parity == 0)[:, None], paired[..., 0], paired[..., 1])


def stat_put(tensor, parity, fill_value):
    filler = jnp.full_like(tensor, fill_value)
    first_half = jnp.where((parity == 0)[:, None], tensor, filler)
    second_half = jnp.where((parity == 1)[:, None], tensor, filler)
    return jnp.stack([first_half, second_half], axis=-1).reshape(
        tensor.shape[:-1] + (2 * tensor.shape[-1],)
    )


def segment_of(positions, lengths):
    seg_ends = jnp.cumsum(lengths)
    return jnp.sum((positions[..., None] >= seg_ends).astype(jnp.int32), axis=-1)


def row_positions(shard_index, tok_dev, stride, offset, row_count):
    return (
        shard_index * tok_dev
        + stride * jnp.arange(row_count, dtype=jnp.int32)[None, :]
        + offset[:, None]
    )


def window_positions(shard_index, distances, tok_dev, stride, offset, row_count):
    return jnp.concatenate(
        [row_positions(shard_index + d, tok_dev, stride, offset, row_count) for d in distances],
        axis=1,
    )


def pair_mask(query_pos, key_pos, lengths, total):
    query_seg = segment_of(query_pos, lengths)
    key_seg = segment_of(key_pos, lengths)
    causal = key_pos[:, None, :] <= query_pos[:, :, None]
    same_seg = key_seg[:, None, :] == query_seg[:, :, None]
    valid = (key_pos[:, None, :] >= 0) & (query_pos[:, :, None] < total)
    return causal & same_seg & valid


def product(pattern, left_operand, right_operand):
    return jnp.einsum(pattern, left_operand, right_operand, preferred_element_type=jnp.float32)


def query_side(shard_index, total, q_rows, g_rows, windows, head_phase, seg_short, seg_long):
    rows_short, head_count, head_width = q_rows.shape
    tok_dev = 2 * rows_short
    scale = 1.0 / math.sqrt(head_width)
    par_short = head_phase % 2
    par_long = head_phase // 2
    levels = [
        (q_rows, g_rows, 2, par_short, seg_short),
        (take_half(q_rows, par_long), take_half(g_rows, par_long), 4, head_phase, seg_long),
    ]
    stored = []
    peaks = []
    for (query_here, grad_here, stride, offset, lengths), (keys, values, key_pos) in zip(levels, windows):
        row_count = query_here.shape[0]
        query_pos = row_positions(shard_index, tok_dev, stride, offset, row_count)
        live = pair_mask(query_pos, key_pos, lengths, total)
        scores = jnp.where(live, product("qhd,khd->hqk", query_here, keys) * scale, VERY_NEGATIVE)
        peaks.append(jnp.max(scores, axis=-1))
        stored.append((live, scores, keys, values))
    top_short = jnp.maximum(peaks[0], stat_put(peaks[1], par_long, VERY_NEGATIVE))
    level_tops = [top_short, stat_half(top_short, par_long)]
    totals = []
    numerators = []
    for level_index, (live, scores, keys, values) in enumerate(stored):
        weights = jnp.where(live, jnp.exp(scores - level_tops[level_index][:, :, None]), 0.0)
        totals.append(jnp.sum(weights, axis=-1))
        numerators.append(product("hqk,khd->qhd", weights.astype(jnp.bfloat16), values))
    denominator = totals[0] + stat_put(totals[1], par_long, 0.0)
    attended = (numerators[0] + put_half(numerators[1], par_long)) / jnp.transpose(denominator)[
        :, :, None
    ]
    delta_rows = jnp.transpose(jnp.sum(g_rows.astype(jnp.float32) * attended, axis=-1))
    inverse = 1.0 / denominator
    level_inverse = [inverse, stat_half(inverse, par_long)]
    level_delta = [delta_rows, stat_half(delta_rows, par_long)]
    grads = []
    for level_index, (live, scores, keys, values) in enumerate(stored):
        grad_here = levels[level_index][1]
        probability = (
            jnp.where(live, jnp.exp(scores - level_tops[level_index][:, :, None]), 0.0)
            * level_inverse[level_index][:, :, None]
        )
        grad_probs = product("qhd,khd->hqk", grad_here, values)
        grad_scores = (probability * (grad_probs - level_delta[level_index][:, :, None])).astype(
            jnp.bfloat16
        )
        grads.append(product("hqk,khd->qhd", grad_scores, keys) * scale)
    grad_query = grads[0] + put_half(grads[1], par_long)
    return grad_query, jnp.stack([top_short, inverse, delta_rows])


def key_side(shard_index, total, k_rows, v_rows, windows, head_phase, seg_short, seg_long):
    rows_short, head_count, head_width = k_rows.shape
    tok_dev = 2 * rows_short
    scale = 1.0 / math.sqrt(head_width)
    par_short = head_phase % 2
    par_long = head_phase // 2
    levels = [
        (k_rows, v_rows, 2, par_short, seg_short),
        (take_half(k_rows, par_long), take_half(v_rows, par_long), 4, head_phase, seg_long),
    ]
    results = []
    for (key_here, value_here, stride, offset, lengths), (queries, grads, row_stats, query_pos) in zip(levels, windows):
        row_count = key_here.shape[0]
        key_pos = row_positions(shard_index, tok_dev, stride, offset, row_count)
        live = pair_mask(query_pos, key_pos, lengths, total)
        scores = jnp.where(live, product("qhd,khd->hqk", queries, key_here) * scale, VERY_NEGATIVE)
        probability = (
            jnp.where(live, jnp.exp(scores - row_stats[0][:, :, None]), 0.0)
            * row_stats[1][:, :, None]
        )
        grad_probs = product("qhd,khd->hqk", grads, value_here)
        grad_scores = (probability * (grad_probs - row_stats[2][:, :, None])).astype(jnp.bfloat16)
        grad_key = product("hqk,qhd->khd", grad_scores, queries) * scale
        grad_value = product("hqk,qhd->khd", probability.astype(jnp.bfloat16), grads)
        results.append((grad_key, grad_value))
    grad_key = results[0][0] + put_half(results[1][0], par_long)
    grad_value = results[0][1] + put_half(results[1][1], par_long)
    return grad_key, grad_value


def shards(
    queries,
    key_vectors,
    value_vectors,
    grad_mixed,
    out_weight,
    head_phase,
    segments_short,
    segments_long,
):
    shard_index = lax.axis_index("seq")
    devices = lax.axis_size("seq")
    tok_dev = queries.shape[1]
    total = devices * tok_dev
    head_count = head_phase.shape[0]
    head_width = queries.shape[2] // head_count
    rows_short = tok_dev // 2
    rows_long = tok_dev // 4
    par_short = head_phase % 2
    par_long = head_phase // 2

    def split_rows(tensor):
        return take_half(tensor.reshape(tok_dev, head_count, head_width), par_short)

    def gathered(tensor):
        return lax.all_gather(tensor, "seq", axis=1, tiled=False)

    near_steps = [d for d in range(1, REACH_SHORT + 1) if d < devices]
    all_long_pos = row_positions(0, tok_dev, 4, head_phase, devices * rows_long)

    own_kv = jnp.stack([split_rows(key_vectors[0]), split_rows(value_vectors[0])])
    all_kv_long = gathered(take_half(own_kv, par_long)).reshape(
        2, devices * rows_long, head_count, head_width
    )
    near_kv = [own_kv] + [passed_along(own_kv, "seq", d) for d in near_steps]
    near_keys = jnp.concatenate([w[0] for w in near_kv], axis=0)
    near_values = jnp.concatenate([w[1] for w in near_kv], axis=0)
    near_key_pos = window_positions(
        shard_index, [-d for d in range(len(near_kv))], tok_dev, 2, par_short, rows_short
    )

    q_rows = split_rows(queries[0])
    grad_out = jnp.einsum(
        "td,rd->tr",
        grad_mixed[0],
        lax.all_gather(out_weight, "fsdp", axis=0, tiled=True),
        preferred_element_type=jnp.float32,
    ).astype(jnp.bfloat16)
    g_rows = split_rows(grad_out)
    own_qg = jnp.stack([q_rows, g_rows])
    all_qg_long = gathered(take_half(own_qg, par_long)).reshape(
        2, devices * rows_long, head_count, head_width
    )
    near_qg = [own_qg] + [passed_along(own_qg, "seq", -d) for d in near_steps]
    near_queries = jnp.concatenate([w[0] for w in near_qg], axis=0)
    near_grads = jnp.concatenate([w[1] for w in near_qg], axis=0)
    near_query_pos = window_positions(
        shard_index, list(range(len(near_qg))), tok_dev, 2, par_short, rows_short
    )

    grad_query, own_stats = query_side(
        shard_index,
        total,
        q_rows,
        g_rows,
        [
            (near_keys, near_values, near_key_pos),
            (all_kv_long[0], all_kv_long[1], all_long_pos),
        ],
        head_phase,
        segments_short,
        segments_long,
    )
    near_stats = [own_stats] + [passed_along(own_stats, "seq", -d) for d in near_steps]
    all_stats_long = lax.all_gather(
        stat_half(own_stats, par_long), "seq", axis=2, tiled=False
    ).reshape(3, head_count, devices * rows_long)
    grad_key, grad_value = key_side(
        shard_index,
        total,
        own_kv[0],
        own_kv[1],
        [
            (near_queries, near_grads, jnp.concatenate(near_stats, axis=-1), near_query_pos),
            (all_qg_long[0], all_qg_long[1], all_stats_long, all_long_pos),
        ],
        head_phase,
        segments_short,
        segments_long,
    )

    def to_tokens(rows_here):
        return put_half(rows_here, par_short).reshape(1, tok_dev, head_count * head_width)

    return (
        to_tokens(grad_query.astype(jnp.bfloat16)),
        to_tokens(grad_key.astype(jnp.bfloat16)),
        to_tokens(grad_value.astype(jnp.bfloat16)),
    )


def solution(mesh):
    placed = (
        P("fsdp", "seq", None),
        P("fsdp", "seq", None),
        P("fsdp", "seq", None),
        P("fsdp", "seq", None),
        P("fsdp", None),
        P(),
        P(),
        P(),
    )
    return jax.shard_map(
        shards,
        mesh=mesh,
        in_specs=placed,
        out_specs=(P("fsdp", "seq", None), P("fsdp", "seq", None), P("fsdp", "seq", None)),
        check_vma=False,
    )
```

```python
import math

import jax
import jax.numpy as jnp
from jax import lax
from jax.sharding import PartitionSpec as P

REACH_SHORT = 4
REACH_LONG = 16


VERY_NEGATIVE = -1e30


def passed_along(value, axis, by):
    devices = lax.axis_size(axis)
    pairs = [(i, i + by) for i in range(devices) if 0 <= i + by < devices]
    return lax.ppermute(value, axis, pairs)


def take_half(tensor, parity):
    layout = tensor.shape
    paired = tensor.reshape(layout[:-3] + (layout[-3] // 2, 2) + layout[-2:])
    return jnp.where((parity == 0)[:, None], paired[..., 0, :, :], paired[..., 1, :, :])


def put_half(tensor, parity):
    zero_fill = jnp.zeros_like(tensor)
    first_half = jnp.where((parity == 0)[:, None], tensor, zero_fill)
    second_half = jnp.where((parity == 1)[:, None], tensor, zero_fill)
    stacked = jnp.stack([first_half, second_half], axis=-3)
    return stacked.reshape(tensor.shape[:-3] + (2 * tensor.shape[-3],) + tensor.shape[-2:])


def stat_half(tensor, parity):
    paired = tensor.reshape(tensor.shape[:-1] + (tensor.shape[-1] // 2, 2))
    return jnp.where((parity == 0)[:, None], paired[..., 0], paired[..., 1])


def stat_put(tensor, parity, fill_value):
    filler = jnp.full_like(tensor, fill_value)
    first_half = jnp.where((parity == 0)[:, None], tensor, filler)
    second_half = jnp.where((parity == 1)[:, None], tensor, filler)
    return jnp.stack([first_half, second_half], axis=-1).reshape(
        tensor.shape[:-1] + (2 * tensor.shape[-1],)
    )


def segment_of(positions, lengths):
    seg_ends = jnp.cumsum(lengths)
    return jnp.sum((positions[..., None] >= seg_ends).astype(jnp.int32), axis=-1)


def row_positions(shard_index, tok_dev, stride, offset, row_count):
    return (
        shard_index * tok_dev
        + stride * jnp.arange(row_count, dtype=jnp.int32)[None, :]
        + offset[:, None]
    )


def window_positions(shard_index, distances, tok_dev, stride, offset, row_count):
    return jnp.concatenate(
        [row_positions(shard_index + d, tok_dev, stride, offset, row_count) for d in distances],
        axis=1,
    )


def pair_mask(query_pos, key_pos, lengths, total):
    query_seg = segment_of(query_pos, lengths)
    key_seg = segment_of(key_pos, lengths)
    causal = key_pos[:, None, :] <= query_pos[:, :, None]
    same_seg = key_seg[:, None, :] == query_seg[:, :, None]
    valid = (key_pos[:, None, :] >= 0) & (query_pos[:, :, None] < total)
    return causal & same_seg & valid


def product(pattern, left_operand, right_operand):
    return jnp.einsum(pattern, left_operand, right_operand, preferred_element_type=jnp.float32)


def query_side(shard_index, total, q_rows, g_rows, windows, head_phase, seg_short, seg_long):
    rows_short, head_count, head_width = q_rows.shape
    tok_dev = 2 * rows_short
    scale = 1.0 / math.sqrt(head_width)
    par_short = head_phase % 2
    par_long = head_phase // 2
    levels = [
        (q_rows, g_rows, 2, par_short, seg_short),
        (take_half(q_rows, par_long), take_half(g_rows, par_long), 4, head_phase, seg_long),
    ]
    stored = []
    peaks = []
    for (query_here, grad_here, stride, offset, lengths), (keys, values, key_pos) in zip(levels, windows):
        row_count = query_here.shape[0]
        query_pos = row_positions(shard_index, tok_dev, stride, offset, row_count)
        live = pair_mask(query_pos, key_pos, lengths, total)
        scores = jnp.where(live, product("qhd,khd->hqk", query_here, keys) * scale, VERY_NEGATIVE)
        peaks.append(jnp.max(scores, axis=-1))
        stored.append((live, scores, keys, values))
    top_short = jnp.maximum(peaks[0], stat_put(peaks[1], par_long, VERY_NEGATIVE))
    level_tops = [top_short, stat_half(top_short, par_long)]
    totals = []
    numerators = []
    for level_index, (live, scores, keys, values) in enumerate(stored):
        weights = jnp.where(live, jnp.exp(scores - level_tops[level_index][:, :, None]), 0.0)
        totals.append(jnp.sum(weights, axis=-1))
        numerators.append(product("hqk,khd->qhd", weights.astype(jnp.bfloat16), values))
    denominator = totals[0] + stat_put(totals[1], par_long, 0.0)
    attended = (numerators[0] + put_half(numerators[1], par_long)) / jnp.transpose(denominator)[
        :, :, None
    ]
    delta_rows = jnp.transpose(jnp.sum(g_rows.astype(jnp.float32) * attended, axis=-1))
    inverse = 1.0 / denominator
    level_inverse = [inverse, stat_half(inverse, par_long)]
    level_delta = [delta_rows, stat_half(delta_rows, par_long)]
    grads = []
    for level_index, (live, scores, keys, values) in enumerate(stored):
        grad_here = levels[level_index][1]
        probability = (
            jnp.where(live, jnp.exp(scores - level_tops[level_index][:, :, None]), 0.0)
            * level_inverse[level_index][:, :, None]
        )
        grad_probs = product("qhd,khd->hqk", grad_here, values)
        grad_scores = (probability * (grad_probs - level_delta[level_index][:, :, None])).astype(
            jnp.bfloat16
        )
        grads.append(product("hqk,khd->qhd", grad_scores, keys) * scale)
    grad_query = grads[0] + put_half(grads[1], par_long)
    return grad_query, jnp.stack([top_short, inverse, delta_rows])


def key_side(shard_index, total, k_rows, v_rows, windows, head_phase, seg_short, seg_long):
    rows_short, head_count, head_width = k_rows.shape
    tok_dev = 2 * rows_short
    scale = 1.0 / math.sqrt(head_width)
    par_short = head_phase % 2
    par_long = head_phase // 2
    levels = [
        (k_rows, v_rows, 2, par_short, seg_short),
        (take_half(k_rows, par_long), take_half(v_rows, par_long), 4, head_phase, seg_long),
    ]
    results = []
    for (key_here, value_here, stride, offset, lengths), (queries, grads, row_stats, query_pos) in zip(levels, windows):
        row_count = key_here.shape[0]
        key_pos = row_positions(shard_index, tok_dev, stride, offset, row_count)
        live = pair_mask(query_pos, key_pos, lengths, total)
        scores = jnp.where(live, product("qhd,khd->hqk", queries, key_here) * scale, VERY_NEGATIVE)
        probability = (
            jnp.where(live, jnp.exp(scores - row_stats[0][:, :, None]), 0.0)
            * row_stats[1][:, :, None]
        )
        grad_probs = product("qhd,khd->hqk", grads, value_here)
        grad_scores = (probability * (grad_probs - row_stats[2][:, :, None])).astype(jnp.bfloat16)
        grad_key = product("hqk,qhd->khd", grad_scores, queries) * scale
        grad_value = product("hqk,qhd->khd", probability.astype(jnp.bfloat16), grads)
        results.append((grad_key, grad_value))
    grad_key = results[0][0] + put_half(results[1][0], par_long)
    grad_value = results[0][1] + put_half(results[1][1], par_long)
    return grad_key, grad_value


def shards(
    queries,
    key_vectors,
    value_vectors,
    grad_mixed,
    out_weight,
    head_phase,
    segments_short,
    segments_long,
):
    shard_index = lax.axis_index("seq")
    devices = lax.axis_size("seq")
    tok_dev = queries.shape[1]
    total = devices * tok_dev
    head_count = head_phase.shape[0]
    head_width = queries.shape[2] // head_count
    rows_short = tok_dev // 2
    rows_long = tok_dev // 4
    par_short = head_phase % 2
    par_long = head_phase // 2

    def split_rows(tensor):
        return take_half(tensor.reshape(tok_dev, head_count, head_width), par_short)

    def gathered(tensor):
        return lax.all_gather(tensor, "seq", axis=1, tiled=False)

    near_steps = [d for d in range(1, REACH_SHORT + 1) if d < devices]
    all_long_pos = row_positions(0, tok_dev, 4, head_phase, devices * rows_long)

    own_kv = jnp.stack([split_rows(key_vectors[0]), split_rows(value_vectors[0])])
    all_kv_long = gathered(take_half(own_kv, par_long)).reshape(
        2, devices * rows_long, head_count, head_width
    )
    near_kv = [own_kv] + [passed_along(own_kv, "seq", d) for d in near_steps]
    near_key_pos = window_positions(
        shard_index, [-d for d in range(len(near_kv))], tok_dev, 2, par_short, rows_short
    )

    q_rows = split_rows(queries[0])
    all_kv_long, near_kv, out_weight = lax.optimization_barrier((all_kv_long, near_kv, out_weight))
    near_keys = jnp.concatenate([w[0] for w in near_kv], axis=0)
    near_values = jnp.concatenate([w[1] for w in near_kv], axis=0)
    grad_out = jnp.einsum(
        "td,rd->tr",
        grad_mixed[0],
        lax.all_gather(out_weight, "fsdp", axis=0, tiled=True),
        preferred_element_type=jnp.float32,
    ).astype(jnp.bfloat16)
    g_rows = split_rows(grad_out)
    own_qg = jnp.stack([q_rows, g_rows])
    all_qg_long = gathered(take_half(own_qg, par_long)).reshape(
        2, devices * rows_long, head_count, head_width
    )
    near_qg = [own_qg] + [passed_along(own_qg, "seq", -d) for d in near_steps]
    near_queries = jnp.concatenate([w[0] for w in near_qg], axis=0)
    near_grads = jnp.concatenate([w[1] for w in near_qg], axis=0)
    near_query_pos = window_positions(
        shard_index, list(range(len(near_qg))), tok_dev, 2, par_short, rows_short
    )

    grad_query, own_stats = query_side(
        shard_index,
        total,
        q_rows,
        g_rows,
        [
            (near_keys, near_values, near_key_pos),
            (all_kv_long[0], all_kv_long[1], all_long_pos),
        ],
        head_phase,
        segments_short,
        segments_long,
    )
    near_stats = [own_stats] + [passed_along(own_stats, "seq", -d) for d in near_steps]
    all_stats_long = lax.all_gather(
        stat_half(own_stats, par_long).reshape(1, -1), "seq", axis=0, tiled=True
    ).reshape(devices, 3, head_count, rows_long)
    all_stats_long = jnp.transpose(all_stats_long, (1, 2, 0, 3)).reshape(
        3, head_count, devices * rows_long
    )
    grad_key, grad_value = key_side(
        shard_index,
        total,
        own_kv[0],
        own_kv[1],
        [
            (near_queries, near_grads, jnp.concatenate(near_stats, axis=-1), near_query_pos),
            (all_qg_long[0], all_qg_long[1], all_stats_long, all_long_pos),
        ],
        head_phase,
        segments_short,
        segments_long,
    )

    def to_tokens(rows_here):
        return put_half(rows_here, par_short).reshape(1, tok_dev, head_count * head_width)

    return (
        to_tokens(grad_query.astype(jnp.bfloat16)),
        to_tokens(grad_key.astype(jnp.bfloat16)),
        to_tokens(grad_value.astype(jnp.bfloat16)),
    )


def solution(mesh):
    placed = (
        P("fsdp", "seq", None),
        P("fsdp", "seq", None),
        P("fsdp", "seq", None),
        P("fsdp", "seq", None),
        P("fsdp", None),
        P(),
        P(),
        P(),
    )
    return jax.shard_map(
        shards,
        mesh=mesh,
        in_specs=placed,
        out_specs=(P("fsdp", "seq", None), P("fsdp", "seq", None), P("fsdp", "seq", None)),
        check_vma=False,
    )
```

```python
import functools
import math

import jax
import jax.numpy as jnp
from jax import lax
from jax.experimental import pallas as pl
from jax.experimental.pallas import tpu as pltpu
from jax.sharding import PartitionSpec as P

REACH_SHORT = 4
REACH_LONG = 16


VERY_NEGATIVE = -1e30


def passed_along(value, axis, by):
    devices = lax.axis_size(axis)
    pairs = [(i, i + by) for i in range(devices) if 0 <= i + by < devices]
    return lax.ppermute(value, axis, pairs)


def take_rows(tensor, parity):
    layout = tensor.shape
    paired = tensor.reshape(layout[:-2] + (layout[-2] // 2, 2, layout[-1]))
    return jnp.where((parity == 0)[:, None, None], paired[..., 0, :], paired[..., 1, :])


def put_rows(tensor, parity):
    zero_fill = jnp.zeros_like(tensor)
    first_half = jnp.where((parity == 0)[:, None, None], tensor, zero_fill)
    second_half = jnp.where((parity == 1)[:, None, None], tensor, zero_fill)
    stacked = jnp.stack([first_half, second_half], axis=-2)
    return stacked.reshape(tensor.shape[:-2] + (2 * tensor.shape[-2], tensor.shape[-1]))


def take_stats(tensor, parity):
    paired = tensor.reshape(tensor.shape[:-1] + (tensor.shape[-1] // 2, 2))
    return jnp.where((parity == 0)[:, None, None], paired[..., 0], paired[..., 1])


def segment_of(positions, lengths):
    seg_ends = jnp.cumsum(lengths)
    return jnp.sum((positions[..., None] >= seg_ends).astype(jnp.int32), axis=-1)


def row_positions(shard_index, tok_dev, stride, offset, row_count):
    return (
        shard_index * tok_dev
        + stride * jnp.arange(row_count, dtype=jnp.int32)[None, :]
        + offset[:, None]
    )


def window_positions(shard_index, distances, tok_dev, stride, offset, row_count):
    return jnp.concatenate(
        [row_positions(shard_index + d, tok_dev, stride, offset, row_count) for d in distances],
        axis=1,
    )


def dot_nt(left, right):
    return lax.dot_general(
        left, right, (((1,), (1,)), ((), ())), preferred_element_type=jnp.float32
    )


def dot_nn(left, right):
    return lax.dot_general(
        left, right, (((1,), (0,)), ((), ())), preferred_element_type=jnp.float32
    )


def query_kernel(
    q_ref, g_ref, ks_ref, vs_ref, kl_ref, vl_ref,
    qpos_ref, qss_ref, qsl_ref, kps_ref, kss_ref, kpl_ref, ksl_ref,
    dq_ref, top_ref, inv_ref, delta_ref, *, scale,
):
    q = q_ref[0]
    g = g_ref[0]
    qpos = qpos_ref[0]
    parts = []
    for k_ref, v_ref, kp_ref, kseg_ref, qseg_ref in (
        (ks_ref, vs_ref, kps_ref, kss_ref, qss_ref),
        (kl_ref, vl_ref, kpl_ref, ksl_ref, qsl_ref),
    ):
        k = k_ref[0]
        live = (kp_ref[0] <= qpos) & (kseg_ref[0] == qseg_ref[0])
        scores = jnp.where(live, dot_nt(q, k) * scale, VERY_NEGATIVE)
        parts.append((live, scores, k, v_ref))
    top = jnp.maximum(
        jnp.max(parts[0][1], axis=1, keepdims=True), jnp.max(parts[1][1], axis=1, keepdims=True)
    )
    total = None
    numer = None
    weights = []
    for live, scores, k, v_ref in parts:
        w = jnp.where(live, jnp.exp(scores - top), 0.0)
        part_total = jnp.sum(w, axis=1, keepdims=True)
        part_numer = dot_nn(w.astype(jnp.bfloat16), v_ref[0])
        total = part_total if total is None else total + part_total
        numer = part_numer if numer is None else numer + part_numer
        weights.append(w)
    attended = numer / total
    delta = jnp.sum(g.astype(jnp.float32) * attended, axis=1, keepdims=True)
    inverse = 1.0 / total
    grad_query = None
    for (live, scores, k, v_ref), w in zip(parts, weights):
        probability = w * inverse
        grad_probs = dot_nt(g, v_ref[0])
        grad_scores = (probability * (grad_probs - delta)).astype(jnp.bfloat16)
        part = dot_nn(grad_scores, k) * scale
        grad_query = part if grad_query is None else grad_query + part
    dq_ref[0] = grad_query
    top_ref[0] = top
    inv_ref[0] = inverse
    delta_ref[0] = delta


def key_kernel(
    k_ref, v_ref, qs_ref, gs_ref, ql_ref, gl_ref,
    kpos_ref, kss_ref, ksl_ref, qps_ref, qss_ref, sts_ref, qpl_ref, qsl_ref, stl_ref,
    dk_ref, dv_ref, *, scale,
):
    k = k_ref[0]
    v = v_ref[0]
    kpos = kpos_ref[0]
    grad_key = None
    grad_value = None
    for q_ref, g_ref, qp_ref, qseg_ref, kseg_ref, st_ref in (
        (qs_ref, gs_ref, qps_ref, qss_ref, kss_ref, sts_ref),
        (ql_ref, gl_ref, qpl_ref, qsl_ref, ksl_ref, stl_ref),
    ):
        q = q_ref[0]
        g = g_ref[0]
        live = (kpos <= qp_ref[0]) & (kseg_ref[0] == qseg_ref[0])
        scores = jnp.where(live, dot_nt(k, q) * scale, VERY_NEGATIVE)
        stats = st_ref[0]
        probability = jnp.where(live, jnp.exp(scores - stats[0:1, :]), 0.0) * stats[1:2, :]
        grad_probs = dot_nt(v, g)
        grad_scores = (probability * (grad_probs - stats[2:3, :])).astype(jnp.bfloat16)
        part_key = dot_nn(grad_scores, q) * scale
        part_value = dot_nn(probability.astype(jnp.bfloat16), g)
        grad_key = part_key if grad_key is None else grad_key + part_key
        grad_value = part_value if grad_value is None else grad_value + part_value
    dk_ref[0] = grad_key
    dv_ref[0] = grad_value


def per_head(shape):
    return pl.BlockSpec((1,) + tuple(shape[1:]), lambda h: (h,) + (0,) * (len(shape) - 1))


def run_per_head(kernel, inputs, out_shapes):
    heads = inputs[0].shape[0]
    return pl.pallas_call(
        kernel,
        grid=(heads,),
        in_specs=[per_head(x.shape) for x in inputs],
        out_specs=[per_head(s.shape) for s in out_shapes],
        out_shape=out_shapes,
        compiler_params=pltpu.CompilerParams(dimension_semantics=("arbitrary",)),
    )(*inputs)


def column(x):
    return x[:, :, None]


def row(x):
    return x[:, None, :]


def shards(
    queries,
    key_vectors,
    value_vectors,
    grad_mixed,
    out_weight,
    head_phase,
    segments_short,
    segments_long,
):
    shard_index = lax.axis_index("seq")
    devices = lax.axis_size("seq")
    tok_dev = queries.shape[1]
    total = devices * tok_dev
    head_count = head_phase.shape[0]
    head_width = queries.shape[2] // head_count
    rows_short = tok_dev // 2
    rows_long = tok_dev // 4
    scale = 1.0 / math.sqrt(head_width)
    par_short = head_phase % 2
    par_long = head_phase // 2

    def split_rows(tensor):
        heads_major = jnp.transpose(tensor.reshape(tok_dev, head_count, head_width), (1, 0, 2))
        return take_rows(heads_major, par_short)

    def gathered(tensor):
        return lax.all_gather(tensor, "seq", axis=2, tiled=True)

    near_steps = [d for d in range(1, REACH_SHORT + 1) if d < devices]
    long_pos = row_positions(0, tok_dev, 4, head_phase, devices * rows_long)
    long_seg = segment_of(long_pos, segments_long)

    own_kv = jnp.stack([split_rows(key_vectors[0]), split_rows(value_vectors[0])])
    all_kv_long = gathered(take_rows(own_kv, par_long))
    near_kv = [own_kv] + [passed_along(own_kv, "seq", d) for d in near_steps]
    near_kv = jnp.concatenate(near_kv, axis=2)

    q_rows = split_rows(queries[0])
    grad_out = jnp.einsum(
        "td,rd->tr",
        grad_mixed[0],
        lax.all_gather(out_weight, "fsdp", axis=0, tiled=True),
        preferred_element_type=jnp.float32,
    ).astype(jnp.bfloat16)
    g_rows = split_rows(grad_out)
    own_qg = jnp.stack([q_rows, g_rows])
    all_qg_long = gathered(take_rows(own_qg, par_long))
    near_qg = [own_qg] + [passed_along(own_qg, "seq", -d) for d in near_steps]
    near_qg = jnp.concatenate(near_qg, axis=2)

    own_pos = row_positions(shard_index, tok_dev, 2, par_short, rows_short)
    own_seg_short = segment_of(own_pos, segments_short)
    own_is_long = (own_pos - head_phase[:, None]) % 4 == 0
    own_seg_long = jnp.where(own_is_long, segment_of(own_pos, segments_long), -3)

    key_pos_short = window_positions(
        shard_index, [-d for d in range(len(near_steps) + 1)], tok_dev, 2, par_short, rows_short
    )
    key_seg_short = jnp.where(key_pos_short >= 0, segment_of(key_pos_short, segments_short), -1)
    f32 = jnp.float32
    row_shape = jax.ShapeDtypeStruct((head_count, rows_short, head_width), f32)
    stat_shape = jax.ShapeDtypeStruct((head_count, rows_short, 1), f32)
    grad_query, top, inverse, delta = run_per_head(
        functools.partial(query_kernel, scale=scale),
        [
            q_rows,
            g_rows,
            near_kv[0],
            near_kv[1],
            all_kv_long[0],
            all_kv_long[1],
            column(own_pos),
            column(own_seg_short),
            column(own_seg_long),
            row(key_pos_short),
            row(key_seg_short),
            row(long_pos),
            row(long_seg),
        ],
        [row_shape, stat_shape, stat_shape, stat_shape],
    )
    own_stats = jnp.stack([top[:, :, 0], inverse[:, :, 0], delta[:, :, 0]], axis=1)
    near_stats = [own_stats] + [passed_along(own_stats, "seq", -d) for d in near_steps]
    near_stats = jnp.concatenate(near_stats, axis=2)
    all_stats_long = lax.all_gather(take_stats(own_stats, par_long), "seq", axis=2, tiled=True)

    query_pos_short = window_positions(
        shard_index, list(range(len(near_steps) + 1)), tok_dev, 2, par_short, rows_short
    )
    query_seg_short = jnp.where(
        query_pos_short < total, segment_of(query_pos_short, segments_short), -2
    )
    grad_key, grad_value = run_per_head(
        functools.partial(key_kernel, scale=scale),
        [
            own_kv[0],
            own_kv[1],
            near_qg[0],
            near_qg[1],
            all_qg_long[0],
            all_qg_long[1],
            column(own_pos),
            column(own_seg_short),
            column(own_seg_long),
            row(query_pos_short),
            row(query_seg_short),
            near_stats,
            row(long_pos),
            row(long_seg),
            all_stats_long,
        ],
        [row_shape, row_shape],
    )

    def to_tokens(rows_here):
        tokens = put_rows(rows_here.astype(jnp.bfloat16), par_short)
        return jnp.transpose(tokens, (1, 0, 2)).reshape(1, tok_dev, head_count * head_width)

    return (to_tokens(grad_query), to_tokens(grad_key), to_tokens(grad_value))


def solution(mesh):
    placed = (
        P("fsdp", "seq", None),
        P("fsdp", "seq", None),
        P("fsdp", "seq", None),
        P("fsdp", "seq", None),
        P("fsdp", None),
        P(),
        P(),
        P(),
    )
    return jax.shard_map(
        shards,
        mesh=mesh,
        in_specs=placed,
        out_specs=(P("fsdp", "seq", None), P("fsdp", "seq", None), P("fsdp", "seq", None)),
        check_vma=False,
    )
```

```python
import functools
import math

import jax
import jax.numpy as jnp
from jax import lax
from jax.experimental import pallas as pl
from jax.experimental.pallas import tpu as pltpu
from jax.sharding import PartitionSpec as P


REACH_SHORT = 4


VERY_NEGATIVE = -1e30


def passed_along(value, axis, by):
    devices = lax.axis_size(axis)
    pairs = [(i, i + by) for i in range(devices) if 0 <= i + by < devices]
    return lax.ppermute(value, axis, pairs)


def take_rows(tensor, parity):
    layout = tensor.shape
    paired = tensor.reshape(layout[:-2] + (layout[-2] // 2, 2, layout[-1]))
    return jnp.where((parity == 0)[:, None, None], paired[..., 0, :], paired[..., 1, :])


def put_rows(tensor, parity):
    zero_fill = jnp.zeros_like(tensor)
    first_half = jnp.where((parity == 0)[:, None, None], tensor, zero_fill)
    second_half = jnp.where((parity == 1)[:, None, None], tensor, zero_fill)
    stacked = jnp.stack([first_half, second_half], axis=-2)
    return stacked.reshape(tensor.shape[:-2] + (2 * tensor.shape[-2], tensor.shape[-1]))


def take_stats(tensor, parity):
    paired = tensor.reshape(tensor.shape[:-1] + (tensor.shape[-1] // 2, 2))
    return jnp.where((parity == 0)[:, None, None], paired[..., 0], paired[..., 1])


def segment_of(positions, lengths):
    seg_ends = jnp.cumsum(lengths)
    return jnp.sum((positions[..., None] >= seg_ends).astype(jnp.int32), axis=-1)


def row_positions(shard_index, tok_dev, stride, offset, row_count):
    return (
        shard_index * tok_dev
        + stride * jnp.arange(row_count, dtype=jnp.int32)[None, :]
        + offset[:, None]
    )


def window_positions(shard_index, distances, tok_dev, stride, offset, row_count):
    return jnp.concatenate(
        [row_positions(shard_index + d, tok_dev, stride, offset, row_count) for d in distances],
        axis=1,
    )


def dot_nt(left, right):
    return lax.dot_general(
        left, right, (((1,), (1,)), ((), ())), preferred_element_type=jnp.float32
    )


def dot_nn(left, right):
    return lax.dot_general(
        left, right, (((1,), (0,)), ((), ())), preferred_element_type=jnp.float32
    )


def query_kernel(
    q_ref, g_ref, ks_ref, vs_ref, kl_ref, vl_ref,
    qpos_ref, qss_ref, qsl_ref, kps_ref, kss_ref, kpl_ref, ksl_ref,
    dq_ref, top_ref, inv_ref, delta_ref, *, scale,
):
    q = q_ref[0]
    g = g_ref[0]
    qpos = qpos_ref[0]
    parts = []
    for k_ref, v_ref, kp_ref, kseg_ref, qseg_ref in (
        (ks_ref, vs_ref, kps_ref, kss_ref, qss_ref),
        (kl_ref, vl_ref, kpl_ref, ksl_ref, qsl_ref),
    ):
        k = k_ref[0]
        live = (kp_ref[0] <= qpos) & (kseg_ref[0] == qseg_ref[0])
        scores = jnp.where(live, dot_nt(q, k) * scale, VERY_NEGATIVE)
        parts.append((live, scores, k, v_ref))
    top = jnp.maximum(
        jnp.max(parts[0][1], axis=1, keepdims=True), jnp.max(parts[1][1], axis=1, keepdims=True)
    )
    total = None
    numer = None
    weights = []
    for live, scores, k, v_ref in parts:
        w = jnp.where(live, jnp.exp(scores - top), 0.0)
        part_total = jnp.sum(w, axis=1, keepdims=True)
        part_numer = dot_nn(w.astype(jnp.bfloat16), v_ref[0])
        total = part_total if total is None else total + part_total
        numer = part_numer if numer is None else numer + part_numer
        weights.append(w)
    attended = numer / total
    delta = jnp.sum(g.astype(jnp.float32) * attended, axis=1, keepdims=True)
    inverse = 1.0 / total
    grad_query = None
    for (live, scores, k, v_ref), w in zip(parts, weights):
        probability = w * inverse
        grad_probs = dot_nt(g, v_ref[0])
        grad_scores = (probability * (grad_probs - delta)).astype(jnp.bfloat16)
        part = dot_nn(grad_scores, k) * scale
        grad_query = part if grad_query is None else grad_query + part
    dq_ref[0] = grad_query
    top_ref[0] = top
    inv_ref[0] = inverse
    delta_ref[0] = delta


def key_kernel(
    k_ref, v_ref, qs_ref, gs_ref, ql_ref, gl_ref,
    kpos_ref, kss_ref, ksl_ref, qps_ref, qss_ref, sts_ref, qpl_ref, qsl_ref, stl_ref,
    dk_ref, dv_ref, *, scale,
):
    k = k_ref[0]
    v = v_ref[0]
    kpos = kpos_ref[0]
    grad_key = None
    grad_value = None
    for q_ref, g_ref, qp_ref, qseg_ref, kseg_ref, st_ref in (
        (qs_ref, gs_ref, qps_ref, qss_ref, kss_ref, sts_ref),
        (ql_ref, gl_ref, qpl_ref, qsl_ref, ksl_ref, stl_ref),
    ):
        q = q_ref[0]
        g = g_ref[0]
        live = (kpos <= qp_ref[0]) & (kseg_ref[0] == qseg_ref[0])
        scores = jnp.where(live, dot_nt(k, q) * scale, VERY_NEGATIVE)
        stats = st_ref[0]
        probability = jnp.where(live, jnp.exp(scores - stats[0:1, :]), 0.0) * stats[1:2, :]
        grad_probs = dot_nt(v, g)
        grad_scores = (probability * (grad_probs - stats[2:3, :])).astype(jnp.bfloat16)
        part_key = dot_nn(grad_scores, q) * scale
        part_value = dot_nn(probability.astype(jnp.bfloat16), g)
        grad_key = part_key if grad_key is None else grad_key + part_key
        grad_value = part_value if grad_value is None else grad_value + part_value
    dk_ref[0] = grad_key
    dv_ref[0] = grad_value


def per_head(shape):
    return pl.BlockSpec((1,) + tuple(shape[1:]), lambda h: (h,) + (0,) * (len(shape) - 1))


def run_per_head(kernel, inputs, out_shapes):
    heads = inputs[0].shape[0]
    return pl.pallas_call(
        kernel,
        grid=(heads,),
        in_specs=[per_head(x.shape) for x in inputs],
        out_specs=[per_head(s.shape) for s in out_shapes],
        out_shape=out_shapes,
        compiler_params=pltpu.CompilerParams(dimension_semantics=("arbitrary",)),
    )(*inputs)


def column(x):
    return x[:, :, None]


def row(x):
    return x[:, None, :]


def shards(
    queries,
    key_vectors,
    value_vectors,
    grad_mixed,
    out_weight,
    head_phase,
    segments_short,
    segments_long,
):
    shard_index = lax.axis_index("seq")
    devices = lax.axis_size("seq")
    tok_dev = queries.shape[1]
    total = devices * tok_dev
    head_count = head_phase.shape[0]
    head_width = queries.shape[2] // head_count
    rows_short = tok_dev // 2
    rows_long = tok_dev // 4
    scale = 1.0 / math.sqrt(head_width)
    par_short = head_phase % 2
    par_long = head_phase // 2

    def split_rows(tensor):
        heads_major = jnp.transpose(tensor.reshape(tok_dev, head_count, head_width), (1, 0, 2))
        return take_rows(heads_major, par_short)

    def gathered(tensor):
        return lax.all_gather(tensor, "seq", axis=2, tiled=True)

    near_steps = [d for d in range(1, REACH_SHORT + 1) if d < devices]
    long_pos = row_positions(0, tok_dev, 4, head_phase, devices * rows_long)
    long_seg = segment_of(long_pos, segments_long)

    own_kv = jnp.stack([split_rows(key_vectors[0]), split_rows(value_vectors[0])])
    all_kv_long = gathered(take_rows(own_kv, par_long))
    near_kv = [own_kv] + [passed_along(own_kv, "seq", d) for d in near_steps]
    near_kv = jnp.concatenate(near_kv, axis=2)

    q_rows = split_rows(queries[0])
    core = shard_index % 2
    half_width = out_weight.shape[1] // 2
    own_half = lax.all_gather(
        lax.dynamic_slice_in_dim(out_weight, core * half_width, half_width, axis=1),
        "fsdp",
        axis=0,
        tiled=True,
    )
    other_half = lax.ppermute(own_half, "seq", [(i, i ^ 1) for i in range(devices)])
    grad_out = jnp.einsum(
        "td,rd->tr",
        lax.dynamic_slice_in_dim(grad_mixed[0], core * half_width, half_width, axis=1),
        own_half,
        preferred_element_type=jnp.float32,
    ) + jnp.einsum(
        "td,rd->tr",
        lax.dynamic_slice_in_dim(grad_mixed[0], (1 - core) * half_width, half_width, axis=1),
        other_half,
        preferred_element_type=jnp.float32,
    )
    grad_out = grad_out.astype(jnp.bfloat16)
    g_rows = split_rows(grad_out)
    own_qg = jnp.stack([q_rows, g_rows])
    all_qg_long = gathered(take_rows(own_qg, par_long))
    near_qg = [own_qg] + [passed_along(own_qg, "seq", -d) for d in near_steps]
    near_qg = jnp.concatenate(near_qg, axis=2)

    own_pos = row_positions(shard_index, tok_dev, 2, par_short, rows_short)
    own_seg_short = segment_of(own_pos, segments_short)
    own_is_long = (own_pos - head_phase[:, None]) % 4 == 0
    own_seg_long = jnp.where(own_is_long, segment_of(own_pos, segments_long), -3)

    key_pos_short = window_positions(
        shard_index, [-d for d in range(len(near_steps) + 1)], tok_dev, 2, par_short, rows_short
    )
    key_seg_short = jnp.where(key_pos_short >= 0, segment_of(key_pos_short, segments_short), -1)
    f32 = jnp.float32
    row_shape = jax.ShapeDtypeStruct((head_count, rows_short, head_width), f32)
    stat_shape = jax.ShapeDtypeStruct((head_count, rows_short, 1), f32)
    grad_query, top, inverse, delta = run_per_head(
        functools.partial(query_kernel, scale=scale),
        [
            q_rows,
            g_rows,
            near_kv[0],
            near_kv[1],
            all_kv_long[0],
            all_kv_long[1],
            column(own_pos),
            column(own_seg_short),
            column(own_seg_long),
            row(key_pos_short),
            row(key_seg_short),
            row(long_pos),
            row(long_seg),
        ],
        [row_shape, stat_shape, stat_shape, stat_shape],
    )
    own_stats = jnp.stack([top[:, :, 0], inverse[:, :, 0], delta[:, :, 0]], axis=1)
    near_stats = [own_stats] + [passed_along(own_stats, "seq", -d) for d in near_steps]
    near_stats = jnp.concatenate(near_stats, axis=2)
    all_stats_long = lax.all_gather(take_stats(own_stats, par_long), "seq", axis=2, tiled=True)

    query_pos_short = window_positions(
        shard_index, list(range(len(near_steps) + 1)), tok_dev, 2, par_short, rows_short
    )
    query_seg_short = jnp.where(
        query_pos_short < total, segment_of(query_pos_short, segments_short), -2
    )
    grad_key, grad_value = run_per_head(
        functools.partial(key_kernel, scale=scale),
        [
            own_kv[0],
            own_kv[1],
            near_qg[0],
            near_qg[1],
            all_qg_long[0],
            all_qg_long[1],
            column(own_pos),
            column(own_seg_short),
            column(own_seg_long),
            row(query_pos_short),
            row(query_seg_short),
            near_stats,
            row(long_pos),
            row(long_seg),
            all_stats_long,
        ],
        [row_shape, row_shape],
    )

    def to_tokens(rows_here):
        tokens = put_rows(rows_here.astype(jnp.bfloat16), par_short)
        return jnp.transpose(tokens, (1, 0, 2)).reshape(1, tok_dev, head_count * head_width)

    return (to_tokens(grad_query), to_tokens(grad_key), to_tokens(grad_value))


def solution(mesh):
    placed = (
        P("fsdp", "seq", None),
        P("fsdp", "seq", None),
        P("fsdp", "seq", None),
        P("fsdp", "seq", None),
        P("fsdp", None),
        P(),
        P(),
        P(),
    )

    return jax.shard_map(
        shards,
        mesh=mesh,
        in_specs=placed,
        out_specs=(P("fsdp", "seq", None), P("fsdp", "seq", None), P("fsdp", "seq", None)),
        check_vma=False,
    )
```

```python
import functools
import math

import jax
import jax.numpy as jnp
from jax import lax
from jax.experimental import pallas as pl
from jax.experimental.pallas import tpu as pltpu
from jax.sharding import PartitionSpec as P


REACH_SHORT = 4


VERY_NEGATIVE = -1e30


def passed_along(value, axis, by):
    devices = lax.axis_size(axis)
    pairs = [(i, i + by) for i in range(devices) if 0 <= i + by < devices]
    return lax.ppermute(value, axis, pairs)


def take_rows(tensor, parity):
    layout = tensor.shape
    paired = tensor.reshape(layout[:-2] + (layout[-2] // 2, 2, layout[-1]))
    return jnp.where((parity == 0)[:, None, None], paired[..., 0, :], paired[..., 1, :])


def put_rows(tensor, parity):
    zero_fill = jnp.zeros_like(tensor)
    first_half = jnp.where((parity == 0)[:, None, None], tensor, zero_fill)
    second_half = jnp.where((parity == 1)[:, None, None], tensor, zero_fill)
    stacked = jnp.stack([first_half, second_half], axis=-2)
    return stacked.reshape(tensor.shape[:-2] + (2 * tensor.shape[-2], tensor.shape[-1]))


def take_stats(tensor, parity):
    paired = tensor.reshape(tensor.shape[:-1] + (tensor.shape[-1] // 2, 2))
    return jnp.where((parity == 0)[:, None, None], paired[..., 0], paired[..., 1])


def segment_of(positions, lengths):
    seg_ends = jnp.cumsum(lengths)
    return jnp.sum((positions[..., None] >= seg_ends).astype(jnp.int32), axis=-1)


def row_positions(shard_index, tok_dev, stride, offset, row_count):
    return (
        shard_index * tok_dev
        + stride * jnp.arange(row_count, dtype=jnp.int32)[None, :]
        + offset[:, None]
    )


def window_positions(shard_index, distances, tok_dev, stride, offset, row_count):
    return jnp.concatenate(
        [row_positions(shard_index + d, tok_dev, stride, offset, row_count) for d in distances],
        axis=1,
    )


def dot_nt(left, right):
    return lax.dot_general(
        left, right, (((1,), (1,)), ((), ())), preferred_element_type=jnp.float32
    )


def dot_nn(left, right):
    return lax.dot_general(
        left, right, (((1,), (0,)), ((), ())), preferred_element_type=jnp.float32
    )


def query_kernel(
    q_ref, g_ref, ks_ref, vs_ref, kl_ref, vl_ref,
    qpos_ref, qss_ref, qsl_ref, kps_ref, kss_ref, kpl_ref, ksl_ref,
    dq_ref, top_ref, inv_ref, delta_ref, *, scale,
):
    q = q_ref[0]
    g = g_ref[0]
    qpos = qpos_ref[0]
    parts = []
    for k_ref, v_ref, kp_ref, kseg_ref, qseg_ref in (
        (ks_ref, vs_ref, kps_ref, kss_ref, qss_ref),
        (kl_ref, vl_ref, kpl_ref, ksl_ref, qsl_ref),
    ):
        k = k_ref[0]
        live = (kp_ref[0] <= qpos) & (kseg_ref[0] == qseg_ref[0])
        scores = jnp.where(live, dot_nt(q, k) * scale, VERY_NEGATIVE)
        parts.append((live, scores, k, v_ref))
    top = jnp.maximum(
        jnp.max(parts[0][1], axis=1, keepdims=True), jnp.max(parts[1][1], axis=1, keepdims=True)
    )
    total = None
    numer = None
    weights = []
    for live, scores, k, v_ref in parts:
        w = jnp.where(live, jnp.exp(scores - top), 0.0)
        part_total = jnp.sum(w, axis=1, keepdims=True)
        part_numer = dot_nn(w.astype(jnp.bfloat16), v_ref[0])
        total = part_total if total is None else total + part_total
        numer = part_numer if numer is None else numer + part_numer
        weights.append(w)
    attended = numer / total
    delta = jnp.sum(g.astype(jnp.float32) * attended, axis=1, keepdims=True)
    inverse = 1.0 / total
    grad_query = None
    for (live, scores, k, v_ref), w in zip(parts, weights):
        probability = w * inverse
        grad_probs = dot_nt(g, v_ref[0])
        grad_scores = (probability * (grad_probs - delta)).astype(jnp.bfloat16)
        part = dot_nn(grad_scores, k) * scale
        grad_query = part if grad_query is None else grad_query + part
    dq_ref[0] = grad_query
    top_ref[0] = top
    inv_ref[0] = inverse
    delta_ref[0] = delta


def key_kernel(
    k_ref, v_ref, qs_ref, gs_ref, ql_ref, gl_ref,
    kpos_ref, kss_ref, ksl_ref, qps_ref, qss_ref, sts_ref, qpl_ref, qsl_ref, stl_ref,
    dk_ref, dv_ref, *, scale,
):
    k = k_ref[0]
    v = v_ref[0]
    kpos = kpos_ref[0]
    grad_key = None
    grad_value = None
    for q_ref, g_ref, qp_ref, qseg_ref, kseg_ref, st_ref in (
        (qs_ref, gs_ref, qps_ref, qss_ref, kss_ref, sts_ref),
        (ql_ref, gl_ref, qpl_ref, qsl_ref, ksl_ref, stl_ref),
    ):
        q = q_ref[0]
        g = g_ref[0]
        live = (kpos <= qp_ref[0]) & (kseg_ref[0] == qseg_ref[0])
        scores = jnp.where(live, dot_nt(k, q) * scale, VERY_NEGATIVE)
        stats = st_ref[0]
        probability = jnp.where(live, jnp.exp(scores - stats[0:1, :]), 0.0) * stats[1:2, :]
        grad_probs = dot_nt(v, g)
        grad_scores = (probability * (grad_probs - stats[2:3, :])).astype(jnp.bfloat16)
        part_key = dot_nn(grad_scores, q) * scale
        part_value = dot_nn(probability.astype(jnp.bfloat16), g)
        grad_key = part_key if grad_key is None else grad_key + part_key
        grad_value = part_value if grad_value is None else grad_value + part_value
    dk_ref[0] = grad_key
    dv_ref[0] = grad_value


def per_head(shape):
    return pl.BlockSpec((1,) + tuple(shape[1:]), lambda h: (h,) + (0,) * (len(shape) - 1))


def run_per_head(kernel, inputs, out_shapes):
    heads = inputs[0].shape[0]
    return pl.pallas_call(
        kernel,
        grid=(heads,),
        in_specs=[per_head(x.shape) for x in inputs],
        out_specs=[per_head(s.shape) for s in out_shapes],
        out_shape=out_shapes,
        compiler_params=pltpu.CompilerParams(dimension_semantics=("arbitrary",)),
    )(*inputs)


def column(x):
    return x[:, :, None]


def row(x):
    return x[:, None, :]


def shards(
    queries,
    key_vectors,
    value_vectors,
    grad_mixed,
    out_weight,
    head_phase,
    segments_short,
    segments_long,
):
    shard_index = lax.axis_index("seq")
    devices = lax.axis_size("seq")
    tok_dev = queries.shape[1]
    total = devices * tok_dev
    head_count = head_phase.shape[0]
    head_width = queries.shape[2] // head_count
    rows_short = tok_dev // 2
    rows_long = tok_dev // 4
    scale = 1.0 / math.sqrt(head_width)
    par_short = head_phase % 2
    par_long = head_phase // 2

    def split_rows(tensor):
        heads_major = jnp.transpose(tensor.reshape(tok_dev, head_count, head_width), (1, 0, 2))
        return take_rows(heads_major, par_short)

    def gathered(tensor):
        return lax.all_gather(tensor, "seq", axis=2, tiled=True)

    near_steps = [d for d in range(1, REACH_SHORT + 1) if d < devices]
    long_pos = row_positions(0, tok_dev, 4, head_phase, devices * rows_long)
    long_seg = segment_of(long_pos, segments_long)

    own_kv = jnp.stack([split_rows(key_vectors[0]), split_rows(value_vectors[0])])
    all_kv_long = gathered(take_rows(own_kv, par_long))
    near_kv = [own_kv] + [passed_along(own_kv, "seq", d) for d in near_steps]
    near_kv = jnp.concatenate(near_kv, axis=2)

    q_rows = split_rows(queries[0])
    core = shard_index % 2
    half_width = out_weight.shape[1] // 2
    own_half = lax.all_gather(
        lax.dynamic_slice_in_dim(out_weight, core * half_width, half_width, axis=1),
        "fsdp",
        axis=0,
        tiled=True,
    )
    other_half = lax.ppermute(own_half, "seq", [(i, i ^ 1) for i in range(devices)])
    grad_out = jnp.einsum(
        "td,rd->tr",
        lax.dynamic_slice_in_dim(grad_mixed[0], core * half_width, half_width, axis=1),
        own_half,
        preferred_element_type=jnp.float32,
    ) + jnp.einsum(
        "td,rd->tr",
        lax.dynamic_slice_in_dim(grad_mixed[0], (1 - core) * half_width, half_width, axis=1),
        other_half,
        preferred_element_type=jnp.float32,
    )
    grad_out = grad_out.astype(jnp.bfloat16)
    g_rows = split_rows(grad_out)
    own_qg = jnp.stack([q_rows, g_rows])
    all_qg_long = gathered(take_rows(own_qg, par_long))
    near_qg = [own_qg] + [passed_along(own_qg, "seq", -d) for d in near_steps]
    near_qg = jnp.concatenate(near_qg, axis=2)

    own_pos = row_positions(shard_index, tok_dev, 2, par_short, rows_short)
    own_seg_short = segment_of(own_pos, segments_short)
    own_is_long = (own_pos - head_phase[:, None]) % 4 == 0
    own_seg_long = jnp.where(own_is_long, segment_of(own_pos, segments_long), -3)

    key_pos_short = window_positions(
        shard_index, [-d for d in range(len(near_steps) + 1)], tok_dev, 2, par_short, rows_short
    )
    key_seg_short = jnp.where(key_pos_short >= 0, segment_of(key_pos_short, segments_short), -1)
    f32 = jnp.float32
    row_shape = jax.ShapeDtypeStruct((head_count, rows_short, head_width), f32)
    stat_shape = jax.ShapeDtypeStruct((head_count, rows_short, 1), f32)
    grad_query, top, inverse, delta = run_per_head(
        functools.partial(query_kernel, scale=scale),
        [
            q_rows,
            g_rows,
            near_kv[0],
            near_kv[1],
            all_kv_long[0],
            all_kv_long[1],
            column(own_pos),
            column(own_seg_short),
            column(own_seg_long),
            row(key_pos_short),
            row(key_seg_short),
            row(long_pos),
            row(long_seg),
        ],
        [row_shape, stat_shape, stat_shape, stat_shape],
    )
    own_stats = jnp.stack([top[:, :, 0], inverse[:, :, 0], delta[:, :, 0]], axis=1)
    all_stats = lax.all_gather(own_stats, "seq", axis=0, tiled=False)
    all_stats_long = take_stats(
        jnp.transpose(all_stats, (1, 2, 0, 3)).reshape(head_count, 3, devices * rows_short),
        par_long,
    )
    spare = jnp.zeros((len(near_steps),) + own_stats.shape, own_stats.dtype)
    near_stats = lax.dynamic_slice_in_dim(
        jnp.concatenate([all_stats, spare], axis=0), shard_index, len(near_steps) + 1, axis=0
    )
    near_stats = jnp.transpose(near_stats, (1, 2, 0, 3)).reshape(
        head_count, 3, (len(near_steps) + 1) * rows_short
    )

    query_pos_short = window_positions(
        shard_index, list(range(len(near_steps) + 1)), tok_dev, 2, par_short, rows_short
    )
    query_seg_short = jnp.where(
        query_pos_short < total, segment_of(query_pos_short, segments_short), -2
    )
    grad_key, grad_value = run_per_head(
        functools.partial(key_kernel, scale=scale),
        [
            own_kv[0],
            own_kv[1],
            near_qg[0],
            near_qg[1],
            all_qg_long[0],
            all_qg_long[1],
            column(own_pos),
            column(own_seg_short),
            column(own_seg_long),
            row(query_pos_short),
            row(query_seg_short),
            near_stats,
            row(long_pos),
            row(long_seg),
            all_stats_long,
        ],
        [row_shape, row_shape],
    )

    def to_tokens(rows_here):
        tokens = put_rows(rows_here.astype(jnp.bfloat16), par_short)
        return jnp.transpose(tokens, (1, 0, 2)).reshape(1, tok_dev, head_count * head_width)

    return (to_tokens(grad_query), to_tokens(grad_key), to_tokens(grad_value))


def solution(mesh):
    placed = (
        P("fsdp", "seq", None),
        P("fsdp", "seq", None),
        P("fsdp", "seq", None),
        P("fsdp", "seq", None),
        P("fsdp", None),
        P(),
        P(),
        P(),
    )

    return jax.shard_map(
        shards,
        mesh=mesh,
        in_specs=placed,
        out_specs=(P("fsdp", "seq", None), P("fsdp", "seq", None), P("fsdp", "seq", None)),
        check_vma=False,
    )
```

```python
import functools
import math

import jax
import jax.numpy as jnp
from jax import lax
from jax.experimental import pallas as pl
from jax.experimental.pallas import tpu as pltpu
from jax.sharding import PartitionSpec as P


REACH_SHORT = 4


VERY_NEGATIVE = -1e30


def passed_along(value, axis, by):
    devices = lax.axis_size(axis)
    pairs = [(i, i + by) for i in range(devices) if 0 <= i + by < devices]
    return lax.ppermute(value, axis, pairs)


def take_rows(tensor, parity):
    layout = tensor.shape
    paired = tensor.reshape(layout[:-2] + (layout[-2] // 2, 2, layout[-1]))
    return jnp.where((parity == 0)[:, None, None], paired[..., 0, :], paired[..., 1, :])


def put_rows(tensor, parity):
    zero_fill = jnp.zeros_like(tensor)
    first_half = jnp.where((parity == 0)[:, None, None], tensor, zero_fill)
    second_half = jnp.where((parity == 1)[:, None, None], tensor, zero_fill)
    stacked = jnp.stack([first_half, second_half], axis=-2)
    return stacked.reshape(tensor.shape[:-2] + (2 * tensor.shape[-2], tensor.shape[-1]))


def take_stats(tensor, parity):
    paired = tensor.reshape(tensor.shape[:-1] + (tensor.shape[-1] // 2, 2))
    return jnp.where((parity == 0)[:, None, None], paired[..., 0], paired[..., 1])


def pick_last(tensor, parity):
    paired = tensor.reshape(tensor.shape[:-1] + (tensor.shape[-1] // 2, 2))
    cond = (parity == 0).reshape((-1,) + (1,) * (tensor.ndim - 1))
    return jnp.where(cond, paired[..., 0], paired[..., 1])


def put_last(tensor, parity):
    cond = (parity == 0).reshape((-1,) + (1,) * (tensor.ndim - 1))
    zero_fill = jnp.zeros_like(tensor)
    stacked = jnp.stack(
        [jnp.where(cond, tensor, zero_fill), jnp.where(cond, zero_fill, tensor)], axis=-1
    )
    return stacked.reshape(tensor.shape[:-1] + (2 * tensor.shape[-1],))


def order_rows(tensor, parity):
    return jnp.concatenate([take_rows(tensor, parity), take_rows(tensor, 1 - parity)], axis=-2)


def unorder_rows(tensor, parity):
    half = tensor.shape[-2] // 2
    return put_rows(tensor[..., :half, :], parity) + put_rows(tensor[..., half:, :], 1 - parity)


def order_last(tensor, parity):
    return jnp.concatenate([pick_last(tensor, parity), pick_last(tensor, 1 - parity)], axis=-1)


def unorder_last(tensor, parity):
    half = tensor.shape[-1] // 2
    return put_last(tensor[..., :half], parity) + put_last(tensor[..., half:], 1 - parity)


def segment_of(positions, lengths):
    seg_ends = jnp.cumsum(lengths)
    return jnp.sum((positions[..., None] >= seg_ends).astype(jnp.int32), axis=-1)


def row_positions(shard_index, tok_dev, stride, offset, row_count):
    return (
        shard_index * tok_dev
        + stride * jnp.arange(row_count, dtype=jnp.int32)[None, :]
        + offset[:, None]
    )


def window_positions(shard_index, distances, tok_dev, stride, offset, row_count):
    return jnp.concatenate(
        [row_positions(shard_index + d, tok_dev, stride, offset, row_count) for d in distances],
        axis=1,
    )


def dot_nt(left, right):
    return lax.dot_general(
        left, right, (((1,), (1,)), ((), ())), preferred_element_type=jnp.float32
    )


def dot_nn(left, right):
    return lax.dot_general(
        left, right, (((1,), (0,)), ((), ())), preferred_element_type=jnp.float32
    )


def attend_rows(q, g, parts, scale):
    scored = [
        (k, v, live, jnp.where(live, dot_nt(q, k) * scale, VERY_NEGATIVE))
        for k, v, live in parts
    ]
    top = None
    for k, v, live, scores in scored:
        part_top = jnp.max(scores, axis=1, keepdims=True)
        top = part_top if top is None else jnp.maximum(top, part_top)
    total = None
    numer = None
    weights = []
    for k, v, live, scores in scored:
        w = jnp.where(live, jnp.exp(scores - top), 0.0)
        part_total = jnp.sum(w, axis=1, keepdims=True)
        part_numer = dot_nn(w.astype(jnp.bfloat16), v)
        total = part_total if total is None else total + part_total
        numer = part_numer if numer is None else numer + part_numer
        weights.append(w)
    attended = numer / total
    delta = jnp.sum(g.astype(jnp.float32) * attended, axis=1, keepdims=True)
    inverse = 1.0 / total
    grad_query = None
    for (k, v, live, scores), w in zip(scored, weights):
        probability = w * inverse
        grad_probs = dot_nt(g, v)
        grad_scores = (probability * (grad_probs - delta)).astype(jnp.bfloat16)
        part = dot_nn(grad_scores, k) * scale
        grad_query = part if grad_query is None else grad_query + part
    return grad_query, top, inverse, delta


def query_kernel(
    q_ref, g_ref, ks_ref, vs_ref, kl_ref, vl_ref,
    qpos_ref, qss_ref, qsl_ref, kps_ref, kss_ref, kpl_ref, ksl_ref,
    dq_ref, top_ref, inv_ref, delta_ref, *, scale,
):
    half = q_ref.shape[1] // 2
    ks = ks_ref[0]
    vs = vs_ref[0]
    for lo, hi, with_long in ((0, half, True), (half, 2 * half, False)):
        q = q_ref[0, lo:hi, :]
        g = g_ref[0, lo:hi, :]
        qpos = qpos_ref[0, lo:hi, :]
        parts = [(ks, vs, (kps_ref[0] <= qpos) & (kss_ref[0] == qss_ref[0, lo:hi, :]))]
        if with_long:
            parts.append(
                (kl_ref[0], vl_ref[0], (kpl_ref[0] <= qpos) & (ksl_ref[0] == qsl_ref[0, lo:hi, :]))
            )
        grad_query, top, inverse, delta = attend_rows(q, g, parts, scale)
        dq_ref[0, lo:hi, :] = grad_query
        top_ref[0, lo:hi, :] = top
        inv_ref[0, lo:hi, :] = inverse
        delta_ref[0, lo:hi, :] = delta


def key_rows(k, v, parts, scale):
    grad_key = None
    grad_value = None
    for q, g, live, stats in parts:
        scores = jnp.where(live, dot_nt(k, q) * scale, VERY_NEGATIVE)
        probability = jnp.where(live, jnp.exp(scores - stats[0:1, :]), 0.0) * stats[1:2, :]
        grad_probs = dot_nt(v, g)
        grad_scores = (probability * (grad_probs - stats[2:3, :])).astype(jnp.bfloat16)
        part_key = dot_nn(grad_scores, q) * scale
        part_value = dot_nn(probability.astype(jnp.bfloat16), g)
        grad_key = part_key if grad_key is None else grad_key + part_key
        grad_value = part_value if grad_value is None else grad_value + part_value
    return grad_key, grad_value


def key_kernel(
    k_ref, v_ref, qs_ref, gs_ref, ql_ref, gl_ref,
    kpos_ref, kss_ref, ksl_ref, qps_ref, qss_ref, sts_ref, qpl_ref, qsl_ref, stl_ref,
    dk_ref, dv_ref, *, scale,
):
    half = k_ref.shape[1] // 2
    qs = qs_ref[0]
    gs = gs_ref[0]
    sts = sts_ref[0]
    for lo, hi, with_long in ((0, half, True), (half, 2 * half, False)):
        k = k_ref[0, lo:hi, :]
        v = v_ref[0, lo:hi, :]
        kpos = kpos_ref[0, lo:hi, :]
        parts = [(qs, gs, (kpos <= qps_ref[0]) & (kss_ref[0, lo:hi, :] == qss_ref[0]), sts)]
        if with_long:
            parts.append(
                (
                    ql_ref[0],
                    gl_ref[0],
                    (kpos <= qpl_ref[0]) & (ksl_ref[0, lo:hi, :] == qsl_ref[0]),
                    stl_ref[0],
                )
            )
        grad_key, grad_value = key_rows(k, v, parts, scale)
        dk_ref[0, lo:hi, :] = grad_key
        dv_ref[0, lo:hi, :] = grad_value


def per_head(shape):
    return pl.BlockSpec((1,) + tuple(shape[1:]), lambda h: (h,) + (0,) * (len(shape) - 1))


def run_per_head(kernel, inputs, out_shapes):
    heads = inputs[0].shape[0]
    return pl.pallas_call(
        kernel,
        grid=(heads,),
        in_specs=[per_head(x.shape) for x in inputs],
        out_specs=[per_head(s.shape) for s in out_shapes],
        out_shape=out_shapes,
        compiler_params=pltpu.CompilerParams(dimension_semantics=("arbitrary",)),
    )(*inputs)


def column(x):
    return x[:, :, None]


def row(x):
    return x[:, None, :]


def shards(
    queries,
    key_vectors,
    value_vectors,
    grad_mixed,
    out_weight,
    head_phase,
    segments_short,
    segments_long,
):
    shard_index = lax.axis_index("seq")
    devices = lax.axis_size("seq")
    tok_dev = queries.shape[1]
    total = devices * tok_dev
    head_count = head_phase.shape[0]
    head_width = queries.shape[2] // head_count
    rows_short = tok_dev // 2
    rows_long = tok_dev // 4
    scale = 1.0 / math.sqrt(head_width)
    par_short = head_phase % 2
    par_long = head_phase // 2

    def split_rows(tensor):
        heads_major = jnp.transpose(tensor.reshape(tok_dev, head_count, head_width), (1, 0, 2))
        return take_rows(heads_major, par_short)

    def gathered(tensor):
        return lax.all_gather(tensor, "seq", axis=2, tiled=True)

    near_steps = [d for d in range(1, REACH_SHORT + 1) if d < devices]
    long_pos = row_positions(0, tok_dev, 4, head_phase, devices * rows_long)
    long_seg = segment_of(long_pos, segments_long)

    own_kv = jnp.stack([split_rows(key_vectors[0]), split_rows(value_vectors[0])])
    all_kv_long = gathered(take_rows(own_kv, par_long))
    near_kv = [own_kv] + [passed_along(own_kv, "seq", d) for d in near_steps]
    near_kv = jnp.concatenate(near_kv, axis=2)

    q_rows = split_rows(queries[0])
    core = shard_index % 2
    half_width = out_weight.shape[1] // 2
    own_half = lax.all_gather(
        lax.dynamic_slice_in_dim(out_weight, core * half_width, half_width, axis=1),
        "fsdp",
        axis=0,
        tiled=True,
    )
    other_half = lax.ppermute(own_half, "seq", [(i, i ^ 1) for i in range(devices)])
    grad_out = jnp.einsum(
        "td,rd->tr",
        lax.dynamic_slice_in_dim(grad_mixed[0], core * half_width, half_width, axis=1),
        own_half,
        preferred_element_type=jnp.float32,
    ) + jnp.einsum(
        "td,rd->tr",
        lax.dynamic_slice_in_dim(grad_mixed[0], (1 - core) * half_width, half_width, axis=1),
        other_half,
        preferred_element_type=jnp.float32,
    )
    grad_out = grad_out.astype(jnp.bfloat16)
    g_rows = split_rows(grad_out)
    own_qg = jnp.stack([q_rows, g_rows])
    all_qg_long = gathered(take_rows(own_qg, par_long))
    near_qg = [own_qg] + [passed_along(own_qg, "seq", -d) for d in near_steps]
    near_qg = jnp.concatenate(near_qg, axis=2)

    own_pos = row_positions(shard_index, tok_dev, 2, par_short, rows_short)
    own_seg_short = segment_of(own_pos, segments_short)
    own_is_long = (own_pos - head_phase[:, None]) % 4 == 0
    own_seg_long = jnp.where(own_is_long, segment_of(own_pos, segments_long), -3)

    key_pos_short = window_positions(
        shard_index, [-d for d in range(len(near_steps) + 1)], tok_dev, 2, par_short, rows_short
    )
    key_seg_short = jnp.where(key_pos_short >= 0, segment_of(key_pos_short, segments_short), -1)
    f32 = jnp.float32
    row_shape = jax.ShapeDtypeStruct((head_count, rows_short, head_width), f32)
    stat_shape = jax.ShapeDtypeStruct((head_count, rows_short, 1), f32)
    grad_query, top, inverse, delta = run_per_head(
        functools.partial(query_kernel, scale=scale),
        [
            order_rows(q_rows, par_long),
            order_rows(g_rows, par_long),
            near_kv[0],
            near_kv[1],
            all_kv_long[0],
            all_kv_long[1],
            column(order_last(own_pos, par_long)),
            column(order_last(own_seg_short, par_long)),
            column(order_last(own_seg_long, par_long)),
            row(key_pos_short),
            row(key_seg_short),
            row(long_pos),
            row(long_seg),
        ],
        [row_shape, stat_shape, stat_shape, stat_shape],
    )
    grad_query = unorder_rows(grad_query, par_long)
    own_stats = unorder_last(
        jnp.stack([top[:, :, 0], inverse[:, :, 0], delta[:, :, 0]], axis=1), par_long
    )
    near_stats = [own_stats] + [passed_along(own_stats, "seq", -d) for d in near_steps]
    near_stats = jnp.concatenate(near_stats, axis=2)
    all_stats_long = lax.all_gather(take_stats(own_stats, par_long), "seq", axis=2, tiled=True)

    query_pos_short = window_positions(
        shard_index, list(range(len(near_steps) + 1)), tok_dev, 2, par_short, rows_short
    )
    query_seg_short = jnp.where(
        query_pos_short < total, segment_of(query_pos_short, segments_short), -2
    )
    grad_key, grad_value = run_per_head(
        functools.partial(key_kernel, scale=scale),
        [
            order_rows(own_kv[0], par_long),
            order_rows(own_kv[1], par_long),
            near_qg[0],
            near_qg[1],
            all_qg_long[0],
            all_qg_long[1],
            column(order_last(own_pos, par_long)),
            column(order_last(own_seg_short, par_long)),
            column(order_last(own_seg_long, par_long)),
            row(query_pos_short),
            row(query_seg_short),
            near_stats,
            row(long_pos),
            row(long_seg),
            all_stats_long,
        ],
        [row_shape, row_shape],
    )
    grad_key = unorder_rows(grad_key, par_long)
    grad_value = unorder_rows(grad_value, par_long)

    def to_tokens(rows_here):
        tokens = put_rows(rows_here.astype(jnp.bfloat16), par_short)
        return jnp.transpose(tokens, (1, 0, 2)).reshape(1, tok_dev, head_count * head_width)

    return (to_tokens(grad_query), to_tokens(grad_key), to_tokens(grad_value))


def solution(mesh):
    placed = (
        P("fsdp", "seq", None),
        P("fsdp", "seq", None),
        P("fsdp", "seq", None),
        P("fsdp", "seq", None),
        P("fsdp", None),
        P(),
        P(),
        P(),
    )

    return jax.shard_map(
        shards,
        mesh=mesh,
        in_specs=placed,
        out_specs=(P("fsdp", "seq", None), P("fsdp", "seq", None), P("fsdp", "seq", None)),
        check_vma=False,
    )
```

```python
import functools
import math

import jax
import jax.numpy as jnp
from jax import lax
from jax.experimental import pallas as pl
from jax.experimental.pallas import tpu as pltpu
from jax.sharding import PartitionSpec as P


REACH_SHORT = 4


VERY_NEGATIVE = -1e30


def passed_along(value, axis, by):
    devices = lax.axis_size(axis)
    pairs = [(i, i + by) for i in range(devices) if 0 <= i + by < devices]
    return lax.ppermute(value, axis, pairs)


def take_rows(tensor, parity):
    layout = tensor.shape
    paired = tensor.reshape(layout[:-2] + (layout[-2] // 2, 2, layout[-1]))
    return jnp.where((parity == 0)[:, None, None], paired[..., 0, :], paired[..., 1, :])


def put_rows(tensor, parity):
    zero_fill = jnp.zeros_like(tensor)
    first_half = jnp.where((parity == 0)[:, None, None], tensor, zero_fill)
    second_half = jnp.where((parity == 1)[:, None, None], tensor, zero_fill)
    stacked = jnp.stack([first_half, second_half], axis=-2)
    return stacked.reshape(tensor.shape[:-2] + (2 * tensor.shape[-2], tensor.shape[-1]))


def take_stats(tensor, parity):
    paired = tensor.reshape(tensor.shape[:-1] + (tensor.shape[-1] // 2, 2))
    return jnp.where((parity == 0)[:, None, None], paired[..., 0], paired[..., 1])


def pick_last(tensor, parity):
    paired = tensor.reshape(tensor.shape[:-1] + (tensor.shape[-1] // 2, 2))
    cond = (parity == 0).reshape((-1,) + (1,) * (tensor.ndim - 1))
    return jnp.where(cond, paired[..., 0], paired[..., 1])


def put_last(tensor, parity):
    cond = (parity == 0).reshape((-1,) + (1,) * (tensor.ndim - 1))
    zero_fill = jnp.zeros_like(tensor)
    stacked = jnp.stack(
        [jnp.where(cond, tensor, zero_fill), jnp.where(cond, zero_fill, tensor)], axis=-1
    )
    return stacked.reshape(tensor.shape[:-1] + (2 * tensor.shape[-1],))


def order_rows(tensor, parity):
    return jnp.concatenate([take_rows(tensor, parity), take_rows(tensor, 1 - parity)], axis=-2)


def unorder_rows(tensor, parity):
    half = tensor.shape[-2] // 2
    return put_rows(tensor[..., :half, :], parity) + put_rows(tensor[..., half:, :], 1 - parity)


def order_last(tensor, parity):
    return jnp.concatenate([pick_last(tensor, parity), pick_last(tensor, 1 - parity)], axis=-1)


def unorder_last(tensor, parity):
    half = tensor.shape[-1] // 2
    return put_last(tensor[..., :half], parity) + put_last(tensor[..., half:], 1 - parity)


def segment_of(positions, lengths):
    seg_ends = jnp.cumsum(lengths)
    return jnp.sum((positions[..., None] >= seg_ends).astype(jnp.int32), axis=-1)


def row_positions(shard_index, tok_dev, stride, offset, row_count):
    return (
        shard_index * tok_dev
        + stride * jnp.arange(row_count, dtype=jnp.int32)[None, :]
        + offset[:, None]
    )


def window_positions(shard_index, distances, tok_dev, stride, offset, row_count):
    return jnp.concatenate(
        [row_positions(shard_index + d, tok_dev, stride, offset, row_count) for d in distances],
        axis=1,
    )


def dot_nt(left, right):
    return lax.dot_general(
        left, right, (((1,), (1,)), ((), ())), preferred_element_type=jnp.float32
    )


def dot_nn(left, right):
    return lax.dot_general(
        left, right, (((1,), (0,)), ((), ())), preferred_element_type=jnp.float32
    )


def attend_rows(q, g, parts, scale):
    scored = [
        (k, v, live, jnp.where(live, dot_nt(q, k) * scale, VERY_NEGATIVE))
        for k, v, live in parts
    ]
    top = None
    for k, v, live, scores in scored:
        part_top = jnp.max(scores, axis=1, keepdims=True)
        top = part_top if top is None else jnp.maximum(top, part_top)
    total = None
    numer = None
    weights = []
    for k, v, live, scores in scored:
        w = jnp.where(live, jnp.exp(scores - top), 0.0)
        part_total = jnp.sum(w, axis=1, keepdims=True)
        part_numer = dot_nn(w.astype(jnp.bfloat16), v)
        total = part_total if total is None else total + part_total
        numer = part_numer if numer is None else numer + part_numer
        weights.append(w)
    attended = numer / total
    delta = jnp.sum(g.astype(jnp.float32) * attended, axis=1, keepdims=True)
    inverse = 1.0 / total
    grad_query = None
    for (k, v, live, scores), w in zip(scored, weights):
        probability = w * inverse
        grad_probs = dot_nt(g, v)
        grad_scores = (probability * (grad_probs - delta)).astype(jnp.bfloat16)
        part = dot_nn(grad_scores, k) * scale
        grad_query = part if grad_query is None else grad_query + part
    return grad_query, top, inverse, delta


def query_kernel(
    q_ref, g_ref, ks_ref, vs_ref, kl_ref, vl_ref,
    qpos_ref, qss_ref, qsl_ref, kps_ref, kss_ref, kpl_ref, ksl_ref,
    dq_ref, top_ref, inv_ref, delta_ref, *, scale,
):
    half = q_ref.shape[1] // 2
    ks = ks_ref[0]
    vs = vs_ref[0]
    for lo, hi, with_long in ((0, half, True), (half, 2 * half, False)):
        q = q_ref[0, lo:hi, :]
        g = g_ref[0, lo:hi, :]
        qpos = qpos_ref[0, lo:hi, :]
        parts = [(ks, vs, (kps_ref[0] <= qpos) & (kss_ref[0] == qss_ref[0, lo:hi, :]))]
        if with_long:
            parts.append(
                (kl_ref[0], vl_ref[0], (kpl_ref[0] <= qpos) & (ksl_ref[0] == qsl_ref[0, lo:hi, :]))
            )
        grad_query, top, inverse, delta = attend_rows(q, g, parts, scale)
        dq_ref[0, lo:hi, :] = grad_query
        top_ref[0, lo:hi, :] = top
        inv_ref[0, lo:hi, :] = inverse
        delta_ref[0, lo:hi, :] = delta


def key_rows(k, v, parts, scale):
    grad_key = None
    grad_value = None
    for q, g, live, stats in parts:
        scores = jnp.where(live, dot_nt(k, q) * scale, VERY_NEGATIVE)
        probability = jnp.where(live, jnp.exp(scores - stats[0:1, :]), 0.0) * stats[1:2, :]
        grad_probs = dot_nt(v, g)
        grad_scores = (probability * (grad_probs - stats[2:3, :])).astype(jnp.bfloat16)
        part_key = dot_nn(grad_scores, q) * scale
        part_value = dot_nn(probability.astype(jnp.bfloat16), g)
        grad_key = part_key if grad_key is None else grad_key + part_key
        grad_value = part_value if grad_value is None else grad_value + part_value
    return grad_key, grad_value


def key_kernel(
    k_ref, v_ref, qs_ref, gs_ref, ql_ref, gl_ref,
    kpos_ref, kss_ref, ksl_ref, qps_ref, qss_ref, sts_ref, qpl_ref, qsl_ref, stl_ref,
    dk_ref, dv_ref, *, scale,
):
    half = k_ref.shape[1] // 2
    qs = qs_ref[0]
    gs = gs_ref[0]
    sts = sts_ref[0]
    for lo, hi, with_long in ((0, half, True), (half, 2 * half, False)):
        k = k_ref[0, lo:hi, :]
        v = v_ref[0, lo:hi, :]
        kpos = kpos_ref[0, lo:hi, :]
        parts = [(qs, gs, (kpos <= qps_ref[0]) & (kss_ref[0, lo:hi, :] == qss_ref[0]), sts)]
        if with_long:
            parts.append(
                (
                    ql_ref[0],
                    gl_ref[0],
                    (kpos <= qpl_ref[0]) & (ksl_ref[0, lo:hi, :] == qsl_ref[0]),
                    stl_ref[0],
                )
            )
        grad_key, grad_value = key_rows(k, v, parts, scale)
        dk_ref[0, lo:hi, :] = grad_key
        dv_ref[0, lo:hi, :] = grad_value


def per_head(shape):
    return pl.BlockSpec((1,) + tuple(shape[1:]), lambda h: (h,) + (0,) * (len(shape) - 1))


def per_head_of(operand):
    if isinstance(operand, tuple):
        stacked, index = operand
        rest = (0,) * (stacked.ndim - 2)
        spec = pl.BlockSpec(
            (pl.Squeezed(), 1) + tuple(stacked.shape[2:]), lambda h: (index, h) + rest
        )
        return spec, stacked
    return per_head(operand.shape), operand


def run_per_head(kernel, inputs, out_shapes):
    heads = out_shapes[0].shape[0]
    specs, arrays = zip(*[per_head_of(x) for x in inputs])
    return pl.pallas_call(
        kernel,
        grid=(heads,),
        in_specs=list(specs),
        out_specs=[per_head(s.shape) for s in out_shapes],
        out_shape=out_shapes,
        compiler_params=pltpu.CompilerParams(dimension_semantics=("arbitrary",)),
    )(*arrays)


def column(x):
    return x[:, :, None]


def row(x):
    return x[:, None, :]


def shards(
    queries,
    key_vectors,
    value_vectors,
    grad_mixed,
    out_weight,
    head_phase,
    segments_short,
    segments_long,
):
    shard_index = lax.axis_index("seq")
    devices = lax.axis_size("seq")
    tok_dev = queries.shape[1]
    total = devices * tok_dev
    head_count = head_phase.shape[0]
    head_width = queries.shape[2] // head_count
    rows_short = tok_dev // 2
    rows_long = tok_dev // 4
    scale = 1.0 / math.sqrt(head_width)
    par_short = head_phase % 2
    par_long = head_phase // 2

    def split_rows(tensor):
        heads_major = jnp.transpose(tensor.reshape(tok_dev, head_count, head_width), (1, 0, 2))
        return take_rows(heads_major, par_short)

    def gathered(tensor):
        return lax.all_gather(tensor, "seq", axis=2, tiled=True)

    near_steps = [d for d in range(1, REACH_SHORT + 1) if d < devices]
    long_pos = row_positions(0, tok_dev, 4, head_phase, devices * rows_long)
    long_seg = segment_of(long_pos, segments_long)

    own_kv = jnp.stack([split_rows(key_vectors[0]), split_rows(value_vectors[0])])
    all_kv_long = gathered(take_rows(own_kv, par_long))
    near_kv = [own_kv] + [passed_along(own_kv, "seq", d) for d in near_steps]
    near_kv = jnp.concatenate(near_kv, axis=2)

    q_rows = split_rows(queries[0])
    core = shard_index % 2
    half_width = out_weight.shape[1] // 2
    own_half = lax.all_gather(
        lax.dynamic_slice_in_dim(out_weight, core * half_width, half_width, axis=1),
        "fsdp",
        axis=0,
        tiled=True,
    )
    other_half = lax.ppermute(own_half, "seq", [(i, i ^ 1) for i in range(devices)])
    grad_out = jnp.einsum(
        "td,rd->tr",
        lax.dynamic_slice_in_dim(grad_mixed[0], core * half_width, half_width, axis=1),
        own_half,
        preferred_element_type=jnp.float32,
    ) + jnp.einsum(
        "td,rd->tr",
        lax.dynamic_slice_in_dim(grad_mixed[0], (1 - core) * half_width, half_width, axis=1),
        other_half,
        preferred_element_type=jnp.float32,
    )
    grad_out = grad_out.astype(jnp.bfloat16)
    g_rows = split_rows(grad_out)
    own_qg = jnp.stack([q_rows, g_rows])
    all_qg_long = gathered(take_rows(own_qg, par_long))
    near_qg = [own_qg] + [passed_along(own_qg, "seq", -d) for d in near_steps]
    near_qg = jnp.concatenate(near_qg, axis=2)

    own_pos = row_positions(shard_index, tok_dev, 2, par_short, rows_short)
    own_seg_short = segment_of(own_pos, segments_short)
    own_is_long = (own_pos - head_phase[:, None]) % 4 == 0
    own_seg_long = jnp.where(own_is_long, segment_of(own_pos, segments_long), -3)

    key_pos_short = window_positions(
        shard_index, [-d for d in range(len(near_steps) + 1)], tok_dev, 2, par_short, rows_short
    )
    key_seg_short = jnp.where(key_pos_short >= 0, segment_of(key_pos_short, segments_short), -1)
    f32 = jnp.float32
    row_shape = jax.ShapeDtypeStruct((head_count, rows_short, head_width), f32)
    stat_shape = jax.ShapeDtypeStruct((head_count, rows_short, 1), f32)
    grad_query, top, inverse, delta = run_per_head(
        functools.partial(query_kernel, scale=scale),
        [
            order_rows(q_rows, par_long),
            order_rows(g_rows, par_long),
            (near_kv, 0),
            (near_kv, 1),
            (all_kv_long, 0),
            (all_kv_long, 1),
            column(order_last(own_pos, par_long)),
            column(order_last(own_seg_short, par_long)),
            column(order_last(own_seg_long, par_long)),
            row(key_pos_short),
            row(key_seg_short),
            row(long_pos),
            row(long_seg),
        ],
        [row_shape, stat_shape, stat_shape, stat_shape],
    )
    grad_query = unorder_rows(grad_query, par_long)
    own_stats = unorder_last(
        jnp.stack([top[:, :, 0], inverse[:, :, 0], delta[:, :, 0]], axis=1), par_long
    )
    near_stats = [own_stats] + [passed_along(own_stats, "seq", -d) for d in near_steps]
    near_stats = jnp.concatenate(near_stats, axis=2)
    all_stats_long = lax.all_gather(take_stats(own_stats, par_long), "seq", axis=2, tiled=True)

    query_pos_short = window_positions(
        shard_index, list(range(len(near_steps) + 1)), tok_dev, 2, par_short, rows_short
    )
    query_seg_short = jnp.where(
        query_pos_short < total, segment_of(query_pos_short, segments_short), -2
    )
    ordered_kv = order_rows(own_kv, par_long)
    grad_key, grad_value = run_per_head(
        functools.partial(key_kernel, scale=scale),
        [
            (ordered_kv, 0),
            (ordered_kv, 1),
            (near_qg, 0),
            (near_qg, 1),
            (all_qg_long, 0),
            (all_qg_long, 1),
            column(order_last(own_pos, par_long)),
            column(order_last(own_seg_short, par_long)),
            column(order_last(own_seg_long, par_long)),
            row(query_pos_short),
            row(query_seg_short),
            near_stats,
            row(long_pos),
            row(long_seg),
            all_stats_long,
        ],
        [row_shape, row_shape],
    )
    grad_key = unorder_rows(grad_key, par_long)
    grad_value = unorder_rows(grad_value, par_long)

    def to_tokens(rows_here):
        tokens = put_rows(rows_here.astype(jnp.bfloat16), par_short)
        return jnp.transpose(tokens, (1, 0, 2)).reshape(1, tok_dev, head_count * head_width)

    return (to_tokens(grad_query), to_tokens(grad_key), to_tokens(grad_value))


def solution(mesh):
    placed = (
        P("fsdp", "seq", None),
        P("fsdp", "seq", None),
        P("fsdp", "seq", None),
        P("fsdp", "seq", None),
        P("fsdp", None),
        P(),
        P(),
        P(),
    )

    return jax.shard_map(
        shards,
        mesh=mesh,
        in_specs=placed,
        out_specs=(P("fsdp", "seq", None), P("fsdp", "seq", None), P("fsdp", "seq", None)),
        check_vma=False,
    )
```

```python
import functools
import math

import jax
import jax.numpy as jnp
from jax import lax
from jax.experimental import pallas as pl
from jax.experimental.pallas import tpu as pltpu
from jax.sharding import PartitionSpec as P


REACH_SHORT = 4


VERY_NEGATIVE = -1e30


def passed_along(value, axis, by):
    devices = lax.axis_size(axis)
    pairs = [(i, i + by) for i in range(devices) if 0 <= i + by < devices]
    return lax.ppermute(value, axis, pairs)


def take_rows(tensor, parity):
    layout = tensor.shape
    paired = tensor.reshape(layout[:-2] + (layout[-2] // 2, 2, layout[-1]))
    return jnp.where((parity == 0)[:, None, None], paired[..., 0, :], paired[..., 1, :])


def put_rows(tensor, parity):
    zero_fill = jnp.zeros_like(tensor)
    first_half = jnp.where((parity == 0)[:, None, None], tensor, zero_fill)
    second_half = jnp.where((parity == 1)[:, None, None], tensor, zero_fill)
    stacked = jnp.stack([first_half, second_half], axis=-2)
    return stacked.reshape(tensor.shape[:-2] + (2 * tensor.shape[-2], tensor.shape[-1]))


def take_stats(tensor, parity):
    paired = tensor.reshape(tensor.shape[:-1] + (tensor.shape[-1] // 2, 2))
    return jnp.where((parity == 0)[:, None, None], paired[..., 0], paired[..., 1])


def pick_last(tensor, parity):
    paired = tensor.reshape(tensor.shape[:-1] + (tensor.shape[-1] // 2, 2))
    cond = (parity == 0).reshape((-1,) + (1,) * (tensor.ndim - 1))
    return jnp.where(cond, paired[..., 0], paired[..., 1])


def put_last(tensor, parity):
    cond = (parity == 0).reshape((-1,) + (1,) * (tensor.ndim - 1))
    zero_fill = jnp.zeros_like(tensor)
    stacked = jnp.stack(
        [jnp.where(cond, tensor, zero_fill), jnp.where(cond, zero_fill, tensor)], axis=-1
    )
    return stacked.reshape(tensor.shape[:-1] + (2 * tensor.shape[-1],))


def order_rows(tensor, parity):
    return jnp.concatenate([take_rows(tensor, parity), take_rows(tensor, 1 - parity)], axis=-2)


def unorder_rows(tensor, parity):
    half = tensor.shape[-2] // 2
    return put_rows(tensor[..., :half, :], parity) + put_rows(tensor[..., half:, :], 1 - parity)


def order_last(tensor, parity):
    return jnp.concatenate([pick_last(tensor, parity), pick_last(tensor, 1 - parity)], axis=-1)


def unorder_last(tensor, parity):
    half = tensor.shape[-1] // 2
    return put_last(tensor[..., :half], parity) + put_last(tensor[..., half:], 1 - parity)


def segment_of(positions, lengths):
    seg_ends = jnp.cumsum(lengths)
    return jnp.sum((positions[..., None] >= seg_ends).astype(jnp.int32), axis=-1)


def row_positions(shard_index, tok_dev, stride, offset, row_count):
    return (
        shard_index * tok_dev
        + stride * jnp.arange(row_count, dtype=jnp.int32)[None, :]
        + offset[:, None]
    )


def window_positions(shard_index, distances, tok_dev, stride, offset, row_count):
    return jnp.concatenate(
        [row_positions(shard_index + d, tok_dev, stride, offset, row_count) for d in distances],
        axis=1,
    )


def dot_nt(left, right):
    return lax.dot_general(
        left, right, (((1,), (1,)), ((), ())), preferred_element_type=jnp.float32
    )


def dot_nn(left, right):
    return lax.dot_general(
        left, right, (((1,), (0,)), ((), ())), preferred_element_type=jnp.float32
    )


def attend_rows(q, g, parts, scale):
    scored = [
        (k, v, live, jnp.where(live, dot_nt(q, k) * scale, VERY_NEGATIVE))
        for k, v, live in parts
    ]
    top = None
    for k, v, live, scores in scored:
        part_top = jnp.max(scores, axis=1, keepdims=True)
        top = part_top if top is None else jnp.maximum(top, part_top)
    total = None
    numer = None
    weights = []
    for k, v, live, scores in scored:
        w = jnp.where(live, jnp.exp(scores - top), 0.0)
        part_total = jnp.sum(w, axis=1, keepdims=True)
        part_numer = dot_nn(w.astype(jnp.bfloat16), v)
        total = part_total if total is None else total + part_total
        numer = part_numer if numer is None else numer + part_numer
        weights.append(w)
    attended = numer / total
    delta = jnp.sum(g.astype(jnp.float32) * attended, axis=1, keepdims=True)
    inverse = 1.0 / total
    grad_query = None
    for (k, v, live, scores), w in zip(scored, weights):
        probability = w * inverse
        grad_probs = dot_nt(g, v)
        grad_scores = (probability * (grad_probs - delta)).astype(jnp.bfloat16)
        part = dot_nn(grad_scores, k) * scale
        grad_query = part if grad_query is None else grad_query + part
    return grad_query, top, inverse, delta


def query_kernel(
    q_ref, g_ref, ks_ref, vs_ref, kl_ref, vl_ref,
    qpos_ref, qss_ref, qsl_ref, kps_ref, kss_ref, kpl_ref, ksl_ref,
    dq_ref, top_ref, inv_ref, delta_ref, *, scale,
):
    half = q_ref.shape[1] // 2
    ks = ks_ref[0]
    vs = vs_ref[0]
    for lo, hi, with_long in ((0, half, True), (half, 2 * half, False)):
        q = q_ref[0, lo:hi, :]
        g = g_ref[0, lo:hi, :]
        qpos = qpos_ref[0, lo:hi, :]
        parts = [(ks, vs, (kps_ref[0] <= qpos) & (kss_ref[0] == qss_ref[0, lo:hi, :]))]
        if with_long:
            parts.append(
                (kl_ref[0], vl_ref[0], (kpl_ref[0] <= qpos) & (ksl_ref[0] == qsl_ref[0, lo:hi, :]))
            )
        grad_query, top, inverse, delta = attend_rows(q, g, parts, scale)
        dq_ref[0, lo:hi, :] = grad_query.astype(dq_ref.dtype)
        top_ref[0, lo:hi, :] = top
        inv_ref[0, lo:hi, :] = inverse
        delta_ref[0, lo:hi, :] = delta


def key_rows(k, v, parts, scale):
    grad_key = None
    grad_value = None
    for q, g, live, stats in parts:
        scores = jnp.where(live, dot_nt(k, q) * scale, VERY_NEGATIVE)
        probability = jnp.where(live, jnp.exp(scores - stats[0:1, :]), 0.0) * stats[1:2, :]
        grad_probs = dot_nt(v, g)
        grad_scores = (probability * (grad_probs - stats[2:3, :])).astype(jnp.bfloat16)
        part_key = dot_nn(grad_scores, q) * scale
        part_value = dot_nn(probability.astype(jnp.bfloat16), g)
        grad_key = part_key if grad_key is None else grad_key + part_key
        grad_value = part_value if grad_value is None else grad_value + part_value
    return grad_key, grad_value


def key_kernel(
    k_ref, v_ref, qs_ref, gs_ref, ql_ref, gl_ref,
    kpos_ref, kss_ref, ksl_ref, qps_ref, qss_ref, sts_ref, qpl_ref, qsl_ref, stl_ref,
    dk_ref, dv_ref, *, scale,
):
    half = k_ref.shape[1] // 2
    qs = qs_ref[0]
    gs = gs_ref[0]
    sts = sts_ref[0]
    for lo, hi, with_long in ((0, half, True), (half, 2 * half, False)):
        k = k_ref[0, lo:hi, :]
        v = v_ref[0, lo:hi, :]
        kpos = kpos_ref[0, lo:hi, :]
        parts = [(qs, gs, (kpos <= qps_ref[0]) & (kss_ref[0, lo:hi, :] == qss_ref[0]), sts)]
        if with_long:
            parts.append(
                (
                    ql_ref[0],
                    gl_ref[0],
                    (kpos <= qpl_ref[0]) & (ksl_ref[0, lo:hi, :] == qsl_ref[0]),
                    stl_ref[0],
                )
            )
        grad_key, grad_value = key_rows(k, v, parts, scale)
        dk_ref[0, lo:hi, :] = grad_key.astype(dk_ref.dtype)
        dv_ref[0, lo:hi, :] = grad_value.astype(dv_ref.dtype)


def per_head(shape):
    return pl.BlockSpec((1,) + tuple(shape[1:]), lambda h: (h,) + (0,) * (len(shape) - 1))


def per_head_of(operand):
    if isinstance(operand, tuple):
        stacked, index = operand
        rest = (0,) * (stacked.ndim - 2)
        spec = pl.BlockSpec(
            (pl.Squeezed(), 1) + tuple(stacked.shape[2:]), lambda h: (index, h) + rest
        )
        return spec, stacked
    return per_head(operand.shape), operand


def run_per_head(kernel, inputs, out_shapes):
    heads = out_shapes[0].shape[0]
    specs, arrays = zip(*[per_head_of(x) for x in inputs])
    return pl.pallas_call(
        kernel,
        grid=(heads,),
        in_specs=list(specs),
        out_specs=[per_head(s.shape) for s in out_shapes],
        out_shape=out_shapes,
        compiler_params=pltpu.CompilerParams(dimension_semantics=("arbitrary",)),
    )(*arrays)


def column(x):
    return x[:, :, None]


def row(x):
    return x[:, None, :]


def shards(
    queries,
    key_vectors,
    value_vectors,
    grad_mixed,
    out_weight,
    head_phase,
    segments_short,
    segments_long,
):
    shard_index = lax.axis_index("seq")
    devices = lax.axis_size("seq")
    tok_dev = queries.shape[1]
    total = devices * tok_dev
    head_count = head_phase.shape[0]
    head_width = queries.shape[2] // head_count
    rows_short = tok_dev // 2
    rows_long = tok_dev // 4
    scale = 1.0 / math.sqrt(head_width)
    par_short = head_phase % 2
    par_long = head_phase // 2

    def split_rows(tensor):
        heads_major = jnp.transpose(tensor.reshape(tok_dev, head_count, head_width), (1, 0, 2))
        return take_rows(heads_major, par_short)

    def gathered(tensor):
        return lax.all_gather(tensor, "seq", axis=2, tiled=True)

    near_steps = [d for d in range(1, REACH_SHORT + 1) if d < devices]
    long_pos = row_positions(0, tok_dev, 4, head_phase, devices * rows_long)
    long_seg = segment_of(long_pos, segments_long)

    own_kv = jnp.stack([split_rows(key_vectors[0]), split_rows(value_vectors[0])])
    all_kv_long = gathered(take_rows(own_kv, par_long))
    near_kv = [own_kv] + [passed_along(own_kv, "seq", d) for d in near_steps]
    near_kv = jnp.concatenate(near_kv, axis=2)

    q_rows = split_rows(queries[0])
    core = shard_index % 2
    half_width = out_weight.shape[1] // 2
    own_half = lax.all_gather(
        lax.dynamic_slice_in_dim(out_weight, core * half_width, half_width, axis=1),
        "fsdp",
        axis=0,
        tiled=True,
    )
    other_half = lax.ppermute(own_half, "seq", [(i, i ^ 1) for i in range(devices)])
    grad_out = jnp.einsum(
        "td,rd->tr",
        lax.dynamic_slice_in_dim(grad_mixed[0], core * half_width, half_width, axis=1),
        own_half,
        preferred_element_type=jnp.float32,
    ) + jnp.einsum(
        "td,rd->tr",
        lax.dynamic_slice_in_dim(grad_mixed[0], (1 - core) * half_width, half_width, axis=1),
        other_half,
        preferred_element_type=jnp.float32,
    )
    grad_out = grad_out.astype(jnp.bfloat16)
    g_rows = split_rows(grad_out)
    own_qg = jnp.stack([q_rows, g_rows])
    all_qg_long = gathered(take_rows(own_qg, par_long))
    near_qg = [own_qg] + [passed_along(own_qg, "seq", -d) for d in near_steps]
    near_qg = jnp.concatenate(near_qg, axis=2)

    own_pos = row_positions(shard_index, tok_dev, 2, par_short, rows_short)
    own_seg_short = segment_of(own_pos, segments_short)
    own_is_long = (own_pos - head_phase[:, None]) % 4 == 0
    own_seg_long = jnp.where(own_is_long, segment_of(own_pos, segments_long), -3)

    key_pos_short = window_positions(
        shard_index, [-d for d in range(len(near_steps) + 1)], tok_dev, 2, par_short, rows_short
    )
    key_seg_short = jnp.where(key_pos_short >= 0, segment_of(key_pos_short, segments_short), -1)
    f32 = jnp.float32
    row_shape = jax.ShapeDtypeStruct((head_count, rows_short, head_width), jnp.bfloat16)
    stat_shape = jax.ShapeDtypeStruct((head_count, rows_short, 1), f32)
    grad_query, top, inverse, delta = run_per_head(
        functools.partial(query_kernel, scale=scale),
        [
            order_rows(q_rows, par_long),
            order_rows(g_rows, par_long),
            (near_kv, 0),
            (near_kv, 1),
            (all_kv_long, 0),
            (all_kv_long, 1),
            column(order_last(own_pos, par_long)),
            column(order_last(own_seg_short, par_long)),
            column(order_last(own_seg_long, par_long)),
            row(key_pos_short),
            row(key_seg_short),
            row(long_pos),
            row(long_seg),
        ],
        [row_shape, stat_shape, stat_shape, stat_shape],
    )
    grad_query = unorder_rows(grad_query, par_long)
    own_stats = unorder_last(
        jnp.stack([top[:, :, 0], inverse[:, :, 0], delta[:, :, 0]], axis=1), par_long
    )
    near_stats = [own_stats] + [passed_along(own_stats, "seq", -d) for d in near_steps]
    near_stats = jnp.concatenate(near_stats, axis=2)
    all_stats_long = lax.all_gather(take_stats(own_stats, par_long), "seq", axis=2, tiled=True)

    query_pos_short = window_positions(
        shard_index, list(range(len(near_steps) + 1)), tok_dev, 2, par_short, rows_short
    )
    query_seg_short = jnp.where(
        query_pos_short < total, segment_of(query_pos_short, segments_short), -2
    )
    ordered_kv = order_rows(own_kv, par_long)
    grad_key, grad_value = run_per_head(
        functools.partial(key_kernel, scale=scale),
        [
            (ordered_kv, 0),
            (ordered_kv, 1),
            (near_qg, 0),
            (near_qg, 1),
            (all_qg_long, 0),
            (all_qg_long, 1),
            column(order_last(own_pos, par_long)),
            column(order_last(own_seg_short, par_long)),
            column(order_last(own_seg_long, par_long)),
            row(query_pos_short),
            row(query_seg_short),
            near_stats,
            row(long_pos),
            row(long_seg),
            all_stats_long,
        ],
        [row_shape, row_shape],
    )
    grad_key = unorder_rows(grad_key, par_long)
    grad_value = unorder_rows(grad_value, par_long)

    def to_tokens(rows_here):
        tokens = put_rows(rows_here.astype(jnp.bfloat16), par_short)
        return jnp.transpose(tokens, (1, 0, 2)).reshape(1, tok_dev, head_count * head_width)

    return (to_tokens(grad_query), to_tokens(grad_key), to_tokens(grad_value))


def solution(mesh):
    placed = (
        P("fsdp", "seq", None),
        P("fsdp", "seq", None),
        P("fsdp", "seq", None),
        P("fsdp", "seq", None),
        P("fsdp", None),
        P(),
        P(),
        P(),
    )

    return jax.shard_map(
        shards,
        mesh=mesh,
        in_specs=placed,
        out_specs=(P("fsdp", "seq", None), P("fsdp", "seq", None), P("fsdp", "seq", None)),
        check_vma=False,
    )
```

```python
import functools
import math

import jax
import jax.numpy as jnp
from jax import lax
from jax.experimental import pallas as pl
from jax.experimental.pallas import tpu as pltpu
from jax.sharding import PartitionSpec as P


REACH_SHORT = 4


VERY_NEGATIVE = -1e30


def passed_along(value, axis, by):
    devices = lax.axis_size(axis)
    pairs = [(i, i + by) for i in range(devices) if 0 <= i + by < devices]
    return lax.ppermute(value, axis, pairs)


def take_rows(tensor, parity):
    layout = tensor.shape
    paired = tensor.reshape(layout[:-2] + (layout[-2] // 2, 2, layout[-1]))
    return jnp.where((parity == 0)[:, None, None], paired[..., 0, :], paired[..., 1, :])


def put_rows(tensor, parity):
    zero_fill = jnp.zeros_like(tensor)
    first_half = jnp.where((parity == 0)[:, None, None], tensor, zero_fill)
    second_half = jnp.where((parity == 1)[:, None, None], tensor, zero_fill)
    stacked = jnp.stack([first_half, second_half], axis=-2)
    return stacked.reshape(tensor.shape[:-2] + (2 * tensor.shape[-2], tensor.shape[-1]))


def take_stats(tensor, parity):
    paired = tensor.reshape(tensor.shape[:-1] + (tensor.shape[-1] // 2, 2))
    return jnp.where((parity == 0)[:, None, None], paired[..., 0], paired[..., 1])


def pick_last(tensor, parity):
    paired = tensor.reshape(tensor.shape[:-1] + (tensor.shape[-1] // 2, 2))
    cond = (parity == 0).reshape((-1,) + (1,) * (tensor.ndim - 1))
    return jnp.where(cond, paired[..., 0], paired[..., 1])


def put_last(tensor, parity):
    cond = (parity == 0).reshape((-1,) + (1,) * (tensor.ndim - 1))
    zero_fill = jnp.zeros_like(tensor)
    stacked = jnp.stack(
        [jnp.where(cond, tensor, zero_fill), jnp.where(cond, zero_fill, tensor)], axis=-1
    )
    return stacked.reshape(tensor.shape[:-1] + (2 * tensor.shape[-1],))


def order_rows(tensor, parity):
    return jnp.concatenate([take_rows(tensor, parity), take_rows(tensor, 1 - parity)], axis=-2)


def unorder_rows(tensor, parity):
    half = tensor.shape[-2] // 2
    return put_rows(tensor[..., :half, :], parity) + put_rows(tensor[..., half:, :], 1 - parity)


def order_last(tensor, parity):
    return jnp.concatenate([pick_last(tensor, parity), pick_last(tensor, 1 - parity)], axis=-1)


def unorder_last(tensor, parity):
    half = tensor.shape[-1] // 2
    return put_last(tensor[..., :half], parity) + put_last(tensor[..., half:], 1 - parity)


def segment_of(positions, lengths):
    seg_ends = jnp.cumsum(lengths)
    return jnp.sum((positions[..., None] >= seg_ends).astype(jnp.int32), axis=-1)


def row_positions(shard_index, tok_dev, stride, offset, row_count):
    return (
        shard_index * tok_dev
        + stride * jnp.arange(row_count, dtype=jnp.int32)[None, :]
        + offset[:, None]
    )


def dot_nt(left, right):
    return lax.dot_general(
        left, right, (((1,), (1,)), ((), ())), preferred_element_type=jnp.float32
    )


def dot_nn(left, right):
    return lax.dot_general(
        left, right, (((1,), (0,)), ((), ())), preferred_element_type=jnp.float32
    )


def attend_rows(q, g, parts, scale):
    scored = [
        (k, v, live, jnp.where(live, dot_nt(q, k) * scale, VERY_NEGATIVE))
        for k, v, live in parts
    ]
    top = None
    for k, v, live, scores in scored:
        part_top = jnp.max(scores, axis=1, keepdims=True)
        top = part_top if top is None else jnp.maximum(top, part_top)
    total = None
    numer = None
    weights = []
    for k, v, live, scores in scored:
        w = jnp.where(live, jnp.exp(scores - top), 0.0)
        part_total = jnp.sum(w, axis=1, keepdims=True)
        part_numer = dot_nn(w.astype(jnp.bfloat16), v)
        total = part_total if total is None else total + part_total
        numer = part_numer if numer is None else numer + part_numer
        weights.append(w)
    attended = numer / total
    delta = jnp.sum(g.astype(jnp.float32) * attended, axis=1, keepdims=True)
    inverse = 1.0 / total
    grad_query = None
    for (k, v, live, scores), w in zip(scored, weights):
        probability = w * inverse
        grad_probs = dot_nt(g, v)
        grad_scores = (probability * (grad_probs - delta)).astype(jnp.bfloat16)
        part = dot_nn(grad_scores, k) * scale
        grad_query = part if grad_query is None else grad_query + part
    return grad_query, top, inverse, delta


def query_kernel(*refs, scale, n_short):
    q_ref, g_ref, qpos_ref, qss_ref, qsl_ref = refs[:5]
    shorts = [refs[5 + 4 * i : 9 + 4 * i] for i in range(n_short)]
    kl_ref, vl_ref, kpl_ref, ksl_ref = refs[5 + 4 * n_short : 9 + 4 * n_short]
    dq_ref, top_ref, inv_ref, delta_ref = refs[9 + 4 * n_short :]
    half = q_ref.shape[1] // 2
    for lo, hi, with_long in ((0, half, True), (half, 2 * half, False)):
        q = q_ref[0, lo:hi, :]
        g = g_ref[0, lo:hi, :]
        qpos = qpos_ref[0, lo:hi, :]
        qseg = qss_ref[0, lo:hi, :]
        parts = [
            (ks_ref[0], vs_ref[0], (kps_ref[0] <= qpos) & (kss_ref[0] == qseg))
            for ks_ref, vs_ref, kps_ref, kss_ref in shorts
        ]
        if with_long:
            parts.append(
                (kl_ref[0], vl_ref[0], (kpl_ref[0] <= qpos) & (ksl_ref[0] == qsl_ref[0, lo:hi, :]))
            )
        grad_query, top, inverse, delta = attend_rows(q, g, parts, scale)
        dq_ref[0, lo:hi, :] = grad_query.astype(dq_ref.dtype)
        top_ref[0, lo:hi, :] = top
        inv_ref[0, lo:hi, :] = inverse
        delta_ref[0, lo:hi, :] = delta


def key_rows(k, v, parts, scale):
    grad_key = None
    grad_value = None
    for q, g, live, stats in parts:
        scores = jnp.where(live, dot_nt(k, q) * scale, VERY_NEGATIVE)
        probability = jnp.where(live, jnp.exp(scores - stats[0:1, :]), 0.0) * stats[1:2, :]
        grad_probs = dot_nt(v, g)
        grad_scores = (probability * (grad_probs - stats[2:3, :])).astype(jnp.bfloat16)
        part_key = dot_nn(grad_scores, q) * scale
        part_value = dot_nn(probability.astype(jnp.bfloat16), g)
        grad_key = part_key if grad_key is None else grad_key + part_key
        grad_value = part_value if grad_value is None else grad_value + part_value
    return grad_key, grad_value


def key_kernel(*refs, scale, n_short):
    k_ref, v_ref, kpos_ref, kss_ref, ksl_ref = refs[:5]
    shorts = [refs[5 + 5 * i : 10 + 5 * i] for i in range(n_short)]
    ql_ref, gl_ref, qpl_ref, qsl_ref, stl_ref = refs[5 + 5 * n_short : 10 + 5 * n_short]
    dk_ref, dv_ref = refs[10 + 5 * n_short :]
    half = k_ref.shape[1] // 2
    for lo, hi, with_long in ((0, half, True), (half, 2 * half, False)):
        k = k_ref[0, lo:hi, :]
        v = v_ref[0, lo:hi, :]
        kpos = kpos_ref[0, lo:hi, :]
        kseg = kss_ref[0, lo:hi, :]
        parts = [
            (qs_ref[0], gs_ref[0], (kpos <= qps_ref[0]) & (kseg == qss_ref[0]), sts_ref[0])
            for qs_ref, gs_ref, qps_ref, qss_ref, sts_ref in shorts
        ]
        if with_long:
            parts.append(
                (
                    ql_ref[0],
                    gl_ref[0],
                    (kpos <= qpl_ref[0]) & (ksl_ref[0, lo:hi, :] == qsl_ref[0]),
                    stl_ref[0],
                )
            )
        grad_key, grad_value = key_rows(k, v, parts, scale)
        dk_ref[0, lo:hi, :] = grad_key.astype(dk_ref.dtype)
        dv_ref[0, lo:hi, :] = grad_value.astype(dv_ref.dtype)


def per_head(shape):
    return pl.BlockSpec((1,) + tuple(shape[1:]), lambda h: (h,) + (0,) * (len(shape) - 1))


def per_head_of(operand):
    if isinstance(operand, tuple):
        stacked, index = operand
        rest = (0,) * (stacked.ndim - 2)
        spec = pl.BlockSpec(
            (pl.Squeezed(), 1) + tuple(stacked.shape[2:]), lambda h: (index, h) + rest
        )
        return spec, stacked
    return per_head(operand.shape), operand


def run_per_head(kernel, inputs, out_shapes):
    heads = out_shapes[0].shape[0]
    specs, arrays = zip(*[per_head_of(x) for x in inputs])
    return pl.pallas_call(
        kernel,
        grid=(heads,),
        in_specs=list(specs),
        out_specs=[per_head(s.shape) for s in out_shapes],
        out_shape=out_shapes,
        compiler_params=pltpu.CompilerParams(dimension_semantics=("arbitrary",)),
    )(*arrays)


def column(x):
    return x[:, :, None]


def row(x):
    return x[:, None, :]


def shards(
    queries,
    key_vectors,
    value_vectors,
    grad_mixed,
    out_weight,
    head_phase,
    segments_short,
    segments_long,
):
    shard_index = lax.axis_index("seq")
    devices = lax.axis_size("seq")
    tok_dev = queries.shape[1]
    total = devices * tok_dev
    head_count = head_phase.shape[0]
    head_width = queries.shape[2] // head_count
    rows_short = tok_dev // 2
    rows_long = tok_dev // 4
    scale = 1.0 / math.sqrt(head_width)
    par_short = head_phase % 2
    par_long = head_phase // 2

    def split_rows(tensor):
        heads_major = jnp.transpose(tensor.reshape(tok_dev, head_count, head_width), (1, 0, 2))
        return take_rows(heads_major, par_short)

    def gathered(tensor):
        return lax.all_gather(tensor, "seq", axis=2, tiled=True)

    near_steps = [d for d in range(1, REACH_SHORT + 1) if d < devices]
    long_pos = row_positions(0, tok_dev, 4, head_phase, devices * rows_long)
    long_seg = segment_of(long_pos, segments_long)

    own_kv = jnp.stack([split_rows(key_vectors[0]), split_rows(value_vectors[0])])
    all_kv_long = gathered(take_rows(own_kv, par_long))
    near_kv = [own_kv] + [passed_along(own_kv, "seq", d) for d in near_steps]

    q_rows = split_rows(queries[0])
    core = shard_index % 2
    half_width = out_weight.shape[1] // 2
    own_half = lax.all_gather(
        lax.dynamic_slice_in_dim(out_weight, core * half_width, half_width, axis=1),
        "fsdp",
        axis=0,
        tiled=True,
    )
    other_half = lax.ppermute(own_half, "seq", [(i, i ^ 1) for i in range(devices)])
    grad_out = jnp.einsum(
        "td,rd->tr",
        lax.dynamic_slice_in_dim(grad_mixed[0], core * half_width, half_width, axis=1),
        own_half,
        preferred_element_type=jnp.float32,
    ) + jnp.einsum(
        "td,rd->tr",
        lax.dynamic_slice_in_dim(grad_mixed[0], (1 - core) * half_width, half_width, axis=1),
        other_half,
        preferred_element_type=jnp.float32,
    )
    grad_out = grad_out.astype(jnp.bfloat16)
    g_rows = split_rows(grad_out)
    own_qg = jnp.stack([q_rows, g_rows])
    all_qg_long = gathered(take_rows(own_qg, par_long))
    near_qg = [own_qg] + [passed_along(own_qg, "seq", -d) for d in near_steps]

    own_pos = row_positions(shard_index, tok_dev, 2, par_short, rows_short)
    own_seg_short = segment_of(own_pos, segments_short)
    own_is_long = (own_pos - head_phase[:, None]) % 4 == 0
    own_seg_long = jnp.where(own_is_long, segment_of(own_pos, segments_long), -3)

    short_keys = []
    for d, window in enumerate(near_kv):
        key_pos = row_positions(shard_index - d, tok_dev, 2, par_short, rows_short)
        key_seg = jnp.where(key_pos >= 0, segment_of(key_pos, segments_short), -1)
        short_keys += [(window, 0), (window, 1), row(key_pos), row(key_seg)]
    ordered_pos = column(order_last(own_pos, par_long))
    ordered_seg_short = column(order_last(own_seg_short, par_long))
    ordered_seg_long = column(order_last(own_seg_long, par_long))
    f32 = jnp.float32
    row_shape = jax.ShapeDtypeStruct((head_count, rows_short, head_width), jnp.bfloat16)
    stat_shape = jax.ShapeDtypeStruct((head_count, rows_short, 1), f32)
    grad_query, top, inverse, delta = run_per_head(
        functools.partial(query_kernel, scale=scale, n_short=len(near_kv)),
        [
            order_rows(q_rows, par_long),
            order_rows(g_rows, par_long),
            ordered_pos,
            ordered_seg_short,
            ordered_seg_long,
        ]
        + short_keys
        + [(all_kv_long, 0), (all_kv_long, 1), row(long_pos), row(long_seg)],
        [row_shape, stat_shape, stat_shape, stat_shape],
    )
    grad_query = unorder_rows(grad_query, par_long)
    own_stats = unorder_last(
        jnp.stack([top[:, :, 0], inverse[:, :, 0], delta[:, :, 0]], axis=1), par_long
    )
    near_stats = [own_stats] + [passed_along(own_stats, "seq", -d) for d in near_steps]
    all_stats_long = lax.all_gather(take_stats(own_stats, par_long), "seq", axis=2, tiled=True)

    short_queries = []
    for d, (window, stats) in enumerate(zip(near_qg, near_stats)):
        query_pos = row_positions(shard_index + d, tok_dev, 2, par_short, rows_short)
        query_seg = jnp.where(query_pos < total, segment_of(query_pos, segments_short), -2)
        short_queries += [(window, 0), (window, 1), row(query_pos), row(query_seg), stats]
    ordered_kv = order_rows(own_kv, par_long)
    grad_key, grad_value = run_per_head(
        functools.partial(key_kernel, scale=scale, n_short=len(near_qg)),
        [(ordered_kv, 0), (ordered_kv, 1), ordered_pos, ordered_seg_short, ordered_seg_long]
        + short_queries
        + [(all_qg_long, 0), (all_qg_long, 1), row(long_pos), row(long_seg), all_stats_long],
        [row_shape, row_shape],
    )
    grad_key = unorder_rows(grad_key, par_long)
    grad_value = unorder_rows(grad_value, par_long)

    def to_tokens(rows_here):
        tokens = put_rows(rows_here.astype(jnp.bfloat16), par_short)
        return jnp.transpose(tokens, (1, 0, 2)).reshape(1, tok_dev, head_count * head_width)

    return (to_tokens(grad_query), to_tokens(grad_key), to_tokens(grad_value))


def solution(mesh):
    placed = (
        P("fsdp", "seq", None),
        P("fsdp", "seq", None),
        P("fsdp", "seq", None),
        P("fsdp", "seq", None),
        P("fsdp", None),
        P(),
        P(),
        P(),
    )

    return jax.shard_map(
        shards,
        mesh=mesh,
        in_specs=placed,
        out_specs=(P("fsdp", "seq", None), P("fsdp", "seq", None), P("fsdp", "seq", None)),
        check_vma=False,
    )
```

```python
import functools
import math

import jax
import jax.numpy as jnp
from jax import lax
from jax.experimental import pallas as pl
from jax.experimental.pallas import tpu as pltpu
from jax.sharding import PartitionSpec as P


REACH_SHORT = 4


VERY_NEGATIVE = -1e30


def passed_along(value, axis, by):
    devices = lax.axis_size(axis)
    pairs = [(i, i + by) for i in range(devices) if 0 <= i + by < devices]
    return lax.ppermute(value, axis, pairs)


def take_rows(tensor, parity):
    layout = tensor.shape
    paired = tensor.reshape(layout[:-2] + (layout[-2] // 2, 2, layout[-1]))
    return jnp.where((parity == 0)[:, None, None], paired[..., 0, :], paired[..., 1, :])


def put_rows(tensor, parity):
    zero_fill = jnp.zeros_like(tensor)
    first_half = jnp.where((parity == 0)[:, None, None], tensor, zero_fill)
    second_half = jnp.where((parity == 1)[:, None, None], tensor, zero_fill)
    stacked = jnp.stack([first_half, second_half], axis=-2)
    return stacked.reshape(tensor.shape[:-2] + (2 * tensor.shape[-2], tensor.shape[-1]))


def take_stats(tensor, parity):
    paired = tensor.reshape(tensor.shape[:-1] + (tensor.shape[-1] // 2, 2))
    return jnp.where((parity == 0)[:, None, None], paired[..., 0], paired[..., 1])


def pick_last(tensor, parity):
    paired = tensor.reshape(tensor.shape[:-1] + (tensor.shape[-1] // 2, 2))
    cond = (parity == 0).reshape((-1,) + (1,) * (tensor.ndim - 1))
    return jnp.where(cond, paired[..., 0], paired[..., 1])


def put_last(tensor, parity):
    cond = (parity == 0).reshape((-1,) + (1,) * (tensor.ndim - 1))
    zero_fill = jnp.zeros_like(tensor)
    stacked = jnp.stack(
        [jnp.where(cond, tensor, zero_fill), jnp.where(cond, zero_fill, tensor)], axis=-1
    )
    return stacked.reshape(tensor.shape[:-1] + (2 * tensor.shape[-1],))


def order_rows(tensor, parity):
    return jnp.concatenate([take_rows(tensor, parity), take_rows(tensor, 1 - parity)], axis=-2)


def unorder_rows(tensor, parity):
    half = tensor.shape[-2] // 2
    return put_rows(tensor[..., :half, :], parity) + put_rows(tensor[..., half:, :], 1 - parity)


def order_last(tensor, parity):
    return jnp.concatenate([pick_last(tensor, parity), pick_last(tensor, 1 - parity)], axis=-1)


def unorder_last(tensor, parity):
    half = tensor.shape[-1] // 2
    return put_last(tensor[..., :half], parity) + put_last(tensor[..., half:], 1 - parity)


def segment_of(positions, lengths):
    seg_ends = jnp.cumsum(lengths)
    return jnp.sum((positions[..., None] >= seg_ends).astype(jnp.int32), axis=-1)


def row_positions(shard_index, tok_dev, stride, offset, row_count):
    return (
        shard_index * tok_dev
        + stride * jnp.arange(row_count, dtype=jnp.int32)[None, :]
        + offset[:, None]
    )


def window_positions(shard_index, distances, tok_dev, stride, offset, row_count):
    return jnp.concatenate(
        [row_positions(shard_index + d, tok_dev, stride, offset, row_count) for d in distances],
        axis=1,
    )


def dot_nt(left, right):
    return lax.dot_general(
        left, right, (((1,), (1,)), ((), ())), preferred_element_type=jnp.float32
    )


def dot_nn(left, right):
    return lax.dot_general(
        left, right, (((1,), (0,)), ((), ())), preferred_element_type=jnp.float32
    )


def attend_rows(q, g, parts, scale):
    scored = [
        (k, v, live, jnp.where(live, dot_nt(q, k) * scale, VERY_NEGATIVE))
        for k, v, live in parts
    ]
    top = None
    for k, v, live, scores in scored:
        part_top = jnp.max(scores, axis=1, keepdims=True)
        top = part_top if top is None else jnp.maximum(top, part_top)
    total = None
    numer = None
    weights = []
    for k, v, live, scores in scored:
        w = jnp.where(live, jnp.exp(scores - top), 0.0)
        part_total = jnp.sum(w, axis=1, keepdims=True)
        part_numer = dot_nn(w.astype(jnp.bfloat16), v)
        total = part_total if total is None else total + part_total
        numer = part_numer if numer is None else numer + part_numer
        weights.append(w)
    attended = numer / total
    delta = jnp.sum(g.astype(jnp.float32) * attended, axis=1, keepdims=True)
    inverse = 1.0 / total
    grad_query = None
    for (k, v, live, scores), w in zip(scored, weights):
        probability = w * inverse
        grad_probs = dot_nt(g, v)
        grad_scores = (probability * (grad_probs - delta)).astype(jnp.bfloat16)
        part = dot_nn(grad_scores, k) * scale
        grad_query = part if grad_query is None else grad_query + part
    return grad_query, top, inverse, delta


def query_kernel(*refs, scale, n_short):
    q_ref, g_ref, qpos_ref, qss_ref, qsl_ref = refs[:5]
    shorts = [refs[5 + 4 * i : 9 + 4 * i] for i in range(n_short)]
    kl_ref, vl_ref, kpl_ref, ksl_ref = refs[5 + 4 * n_short : 9 + 4 * n_short]
    dq_ref, top_ref, inv_ref, delta_ref = refs[9 + 4 * n_short :]
    half = q_ref.shape[1] // 2
    for lo, hi, with_long in ((0, half, True), (half, 2 * half, False)):
        q = q_ref[0, lo:hi, :]
        g = g_ref[0, lo:hi, :]
        qpos = qpos_ref[0, lo:hi, :]
        qseg = qss_ref[0, lo:hi, :]
        parts = [
            (ks_ref[0], vs_ref[0], (kps_ref[0] <= qpos) & (kss_ref[0] == qseg))
            for ks_ref, vs_ref, kps_ref, kss_ref in shorts
        ]
        if with_long:
            parts.append(
                (kl_ref[0], vl_ref[0], (kpl_ref[0] <= qpos) & (ksl_ref[0] == qsl_ref[0, lo:hi, :]))
            )
        grad_query, top, inverse, delta = attend_rows(q, g, parts, scale)
        dq_ref[0, lo:hi, :] = grad_query.astype(dq_ref.dtype)
        top_ref[0, lo:hi, :] = top
        inv_ref[0, lo:hi, :] = inverse
        delta_ref[0, lo:hi, :] = delta


def key_rows(k, v, parts, scale):
    grad_key = None
    grad_value = None
    for q, g, live, stats in parts:
        scores = jnp.where(live, dot_nt(k, q) * scale, VERY_NEGATIVE)
        probability = jnp.where(live, jnp.exp(scores - stats[0:1, :]), 0.0) * stats[1:2, :]
        grad_probs = dot_nt(v, g)
        grad_scores = (probability * (grad_probs - stats[2:3, :])).astype(jnp.bfloat16)
        part_key = dot_nn(grad_scores, q) * scale
        part_value = dot_nn(probability.astype(jnp.bfloat16), g)
        grad_key = part_key if grad_key is None else grad_key + part_key
        grad_value = part_value if grad_value is None else grad_value + part_value
    return grad_key, grad_value


def key_kernel(
    k_ref, v_ref, qs_ref, gs_ref, ql_ref, gl_ref,
    kpos_ref, kss_ref, ksl_ref, qps_ref, qss_ref, sts_ref, qpl_ref, qsl_ref, stl_ref,
    dk_ref, dv_ref, *, scale,
):
    half = k_ref.shape[1] // 2
    qs = qs_ref[0]
    gs = gs_ref[0]
    sts = sts_ref[0]
    for lo, hi, with_long in ((0, half, True), (half, 2 * half, False)):
        k = k_ref[0, lo:hi, :]
        v = v_ref[0, lo:hi, :]
        kpos = kpos_ref[0, lo:hi, :]
        parts = [(qs, gs, (kpos <= qps_ref[0]) & (kss_ref[0, lo:hi, :] == qss_ref[0]), sts)]
        if with_long:
            parts.append(
                (
                    ql_ref[0],
                    gl_ref[0],
                    (kpos <= qpl_ref[0]) & (ksl_ref[0, lo:hi, :] == qsl_ref[0]),
                    stl_ref[0],
                )
            )
        grad_key, grad_value = key_rows(k, v, parts, scale)
        dk_ref[0, lo:hi, :] = grad_key.astype(dk_ref.dtype)
        dv_ref[0, lo:hi, :] = grad_value.astype(dv_ref.dtype)


def per_head(shape):
    return pl.BlockSpec((1,) + tuple(shape[1:]), lambda h: (h,) + (0,) * (len(shape) - 1))


def per_head_of(operand):
    if isinstance(operand, tuple):
        stacked, index = operand
        rest = (0,) * (stacked.ndim - 2)
        spec = pl.BlockSpec(
            (pl.Squeezed(), 1) + tuple(stacked.shape[2:]), lambda h: (index, h) + rest
        )
        return spec, stacked
    return per_head(operand.shape), operand


def run_per_head(kernel, inputs, out_shapes):
    heads = out_shapes[0].shape[0]
    specs, arrays = zip(*[per_head_of(x) for x in inputs])
    return pl.pallas_call(
        kernel,
        grid=(heads,),
        in_specs=list(specs),
        out_specs=[per_head(s.shape) for s in out_shapes],
        out_shape=out_shapes,
        compiler_params=pltpu.CompilerParams(dimension_semantics=("arbitrary",)),
    )(*arrays)


def column(x):
    return x[:, :, None]


def row(x):
    return x[:, None, :]


def shards(
    queries,
    key_vectors,
    value_vectors,
    grad_mixed,
    out_weight,
    head_phase,
    segments_short,
    segments_long,
):
    shard_index = lax.axis_index("seq")
    devices = lax.axis_size("seq")
    tok_dev = queries.shape[1]
    total = devices * tok_dev
    head_count = head_phase.shape[0]
    head_width = queries.shape[2] // head_count
    rows_short = tok_dev // 2
    rows_long = tok_dev // 4
    scale = 1.0 / math.sqrt(head_width)
    par_short = head_phase % 2
    par_long = head_phase // 2

    def split_rows(tensor):
        heads_major = jnp.transpose(tensor.reshape(tok_dev, head_count, head_width), (1, 0, 2))
        return take_rows(heads_major, par_short)

    def gathered(tensor):
        return lax.all_gather(tensor, "seq", axis=2, tiled=True)

    near_steps = [d for d in range(1, REACH_SHORT + 1) if d < devices]
    long_pos = row_positions(0, tok_dev, 4, head_phase, devices * rows_long)
    long_seg = segment_of(long_pos, segments_long)

    own_kv = jnp.stack([split_rows(key_vectors[0]), split_rows(value_vectors[0])])
    all_kv_long = gathered(take_rows(own_kv, par_long))
    near_kv = [own_kv] + [passed_along(own_kv, "seq", d) for d in near_steps]

    q_rows = split_rows(queries[0])
    core = shard_index % 2
    half_width = out_weight.shape[1] // 2
    own_half = lax.all_gather(
        lax.dynamic_slice_in_dim(out_weight, core * half_width, half_width, axis=1),
        "fsdp",
        axis=0,
        tiled=True,
    )
    other_half = lax.ppermute(own_half, "seq", [(i, i ^ 1) for i in range(devices)])
    grad_out = jnp.einsum(
        "td,rd->tr",
        lax.dynamic_slice_in_dim(grad_mixed[0], core * half_width, half_width, axis=1),
        own_half,
        preferred_element_type=jnp.float32,
    ) + jnp.einsum(
        "td,rd->tr",
        lax.dynamic_slice_in_dim(grad_mixed[0], (1 - core) * half_width, half_width, axis=1),
        other_half,
        preferred_element_type=jnp.float32,
    )
    grad_out = grad_out.astype(jnp.bfloat16)
    g_rows = split_rows(grad_out)
    own_qg = jnp.stack([q_rows, g_rows])
    all_qg_long = gathered(take_rows(own_qg, par_long))
    near_qg = [own_qg] + [passed_along(own_qg, "seq", -d) for d in near_steps]
    near_qg = jnp.concatenate(near_qg, axis=2)

    own_pos = row_positions(shard_index, tok_dev, 2, par_short, rows_short)
    own_seg_short = segment_of(own_pos, segments_short)
    own_is_long = (own_pos - head_phase[:, None]) % 4 == 0
    own_seg_long = jnp.where(own_is_long, segment_of(own_pos, segments_long), -3)

    short_keys = []
    for d, window in enumerate(near_kv):
        key_pos = row_positions(shard_index - d, tok_dev, 2, par_short, rows_short)
        key_seg = jnp.where(key_pos >= 0, segment_of(key_pos, segments_short), -1)
        short_keys += [(window, 0), (window, 1), row(key_pos), row(key_seg)]
    f32 = jnp.float32
    row_shape = jax.ShapeDtypeStruct((head_count, rows_short, head_width), jnp.bfloat16)
    stat_shape = jax.ShapeDtypeStruct((head_count, rows_short, 1), f32)
    grad_query, top, inverse, delta = run_per_head(
        functools.partial(query_kernel, scale=scale, n_short=len(near_kv)),
        [
            order_rows(q_rows, par_long),
            order_rows(g_rows, par_long),
            column(order_last(own_pos, par_long)),
            column(order_last(own_seg_short, par_long)),
            column(order_last(own_seg_long, par_long)),
        ]
        + short_keys
        + [(all_kv_long, 0), (all_kv_long, 1), row(long_pos), row(long_seg)],
        [row_shape, stat_shape, stat_shape, stat_shape],
    )
    grad_query = unorder_rows(grad_query, par_long)
    own_stats = unorder_last(
        jnp.stack([top[:, :, 0], inverse[:, :, 0], delta[:, :, 0]], axis=1), par_long
    )
    all_stats = lax.all_gather(own_stats, "seq", axis=2, tiled=True)
    all_stats_long = take_stats(all_stats, par_long)
    spare = jnp.zeros(own_stats.shape[:2] + (len(near_steps) * rows_short,), own_stats.dtype)
    near_stats = lax.dynamic_slice_in_dim(
        jnp.concatenate([all_stats, spare], axis=2),
        shard_index * rows_short,
        (len(near_steps) + 1) * rows_short,
        axis=2,
    )

    query_pos_short = window_positions(
        shard_index, list(range(len(near_steps) + 1)), tok_dev, 2, par_short, rows_short
    )
    query_seg_short = jnp.where(
        query_pos_short < total, segment_of(query_pos_short, segments_short), -2
    )
    ordered_kv = order_rows(own_kv, par_long)
    grad_key, grad_value = run_per_head(
        functools.partial(key_kernel, scale=scale),
        [
            (ordered_kv, 0),
            (ordered_kv, 1),
            (near_qg, 0),
            (near_qg, 1),
            (all_qg_long, 0),
            (all_qg_long, 1),
            column(order_last(own_pos, par_long)),
            column(order_last(own_seg_short, par_long)),
            column(order_last(own_seg_long, par_long)),
            row(query_pos_short),
            row(query_seg_short),
            near_stats,
            row(long_pos),
            row(long_seg),
            all_stats_long,
        ],
        [row_shape, row_shape],
    )
    grad_key = unorder_rows(grad_key, par_long)
    grad_value = unorder_rows(grad_value, par_long)

    def to_tokens(rows_here):
        tokens = put_rows(rows_here.astype(jnp.bfloat16), par_short)
        return jnp.transpose(tokens, (1, 0, 2)).reshape(1, tok_dev, head_count * head_width)

    return (to_tokens(grad_query), to_tokens(grad_key), to_tokens(grad_value))


def solution(mesh):
    placed = (
        P("fsdp", "seq", None),
        P("fsdp", "seq", None),
        P("fsdp", "seq", None),
        P("fsdp", "seq", None),
        P("fsdp", None),
        P(),
        P(),
        P(),
    )

    return jax.shard_map(
        shards,
        mesh=mesh,
        in_specs=placed,
        out_specs=(P("fsdp", "seq", None), P("fsdp", "seq", None), P("fsdp", "seq", None)),
        check_vma=False,
    )
```

```python
import functools
import math

import jax
import jax.numpy as jnp
from jax import lax
from jax.experimental import pallas as pl
from jax.experimental.pallas import tpu as pltpu
from jax.sharding import PartitionSpec as P


REACH_SHORT = 4


VERY_NEGATIVE = -1e30


def passed_along(value, axis, by):
    devices = lax.axis_size(axis)
    pairs = [(i, i + by) for i in range(devices) if 0 <= i + by < devices]
    return lax.ppermute(value, axis, pairs)


def take_rows(tensor, parity):
    layout = tensor.shape
    paired = tensor.reshape(layout[:-2] + (layout[-2] // 2, 2, layout[-1]))
    return jnp.where((parity == 0)[:, None, None], paired[..., 0, :], paired[..., 1, :])


def put_rows(tensor, parity):
    zero_fill = jnp.zeros_like(tensor)
    first_half = jnp.where((parity == 0)[:, None, None], tensor, zero_fill)
    second_half = jnp.where((parity == 1)[:, None, None], tensor, zero_fill)
    stacked = jnp.stack([first_half, second_half], axis=-2)
    return stacked.reshape(tensor.shape[:-2] + (2 * tensor.shape[-2], tensor.shape[-1]))


def take_stats(tensor, parity):
    paired = tensor.reshape(tensor.shape[:-1] + (tensor.shape[-1] // 2, 2))
    return jnp.where((parity == 0)[:, None, None], paired[..., 0], paired[..., 1])


def pick_last(tensor, parity):
    paired = tensor.reshape(tensor.shape[:-1] + (tensor.shape[-1] // 2, 2))
    cond = (parity == 0).reshape((-1,) + (1,) * (tensor.ndim - 1))
    return jnp.where(cond, paired[..., 0], paired[..., 1])


def put_last(tensor, parity):
    cond = (parity == 0).reshape((-1,) + (1,) * (tensor.ndim - 1))
    zero_fill = jnp.zeros_like(tensor)
    stacked = jnp.stack(
        [jnp.where(cond, tensor, zero_fill), jnp.where(cond, zero_fill, tensor)], axis=-1
    )
    return stacked.reshape(tensor.shape[:-1] + (2 * tensor.shape[-1],))


def order_rows(tensor, parity):
    return jnp.concatenate([take_rows(tensor, parity), take_rows(tensor, 1 - parity)], axis=-2)


def unorder_rows(tensor, parity):
    half = tensor.shape[-2] // 2
    return put_rows(tensor[..., :half, :], parity) + put_rows(tensor[..., half:, :], 1 - parity)


def order_last(tensor, parity):
    return jnp.concatenate([pick_last(tensor, parity), pick_last(tensor, 1 - parity)], axis=-1)


def unorder_last(tensor, parity):
    half = tensor.shape[-1] // 2
    return put_last(tensor[..., :half], parity) + put_last(tensor[..., half:], 1 - parity)


def segment_of(positions, lengths):
    seg_ends = jnp.cumsum(lengths)
    return jnp.sum((positions[..., None] >= seg_ends).astype(jnp.int32), axis=-1)


def row_positions(shard_index, tok_dev, stride, offset, row_count):
    return (
        shard_index * tok_dev
        + stride * jnp.arange(row_count, dtype=jnp.int32)[None, :]
        + offset[:, None]
    )


def window_positions(shard_index, distances, tok_dev, stride, offset, row_count):
    return jnp.concatenate(
        [row_positions(shard_index + d, tok_dev, stride, offset, row_count) for d in distances],
        axis=1,
    )


def dot_nt(left, right):
    return lax.dot_general(
        left, right, (((1,), (1,)), ((), ())), preferred_element_type=jnp.float32
    )


def dot_nn(left, right):
    return lax.dot_general(
        left, right, (((1,), (0,)), ((), ())), preferred_element_type=jnp.float32
    )


def attend_rows(q, g, parts, scale):
    scored = [
        (k, v, live, jnp.where(live, dot_nt(q, k) * scale, VERY_NEGATIVE))
        for k, v, live in parts
    ]
    top = None
    for k, v, live, scores in scored:
        part_top = jnp.max(scores, axis=1, keepdims=True)
        top = part_top if top is None else jnp.maximum(top, part_top)
    total = None
    numer = None
    weights = []
    for k, v, live, scores in scored:
        w = jnp.where(live, jnp.exp(scores - top), 0.0)
        part_total = jnp.sum(w, axis=1, keepdims=True)
        part_numer = dot_nn(w.astype(jnp.bfloat16), v)
        total = part_total if total is None else total + part_total
        numer = part_numer if numer is None else numer + part_numer
        weights.append(w)
    attended = numer / total
    delta = jnp.sum(g.astype(jnp.float32) * attended, axis=1, keepdims=True)
    inverse = 1.0 / total
    grad_query = None
    for (k, v, live, scores), w in zip(scored, weights):
        probability = w * inverse
        grad_probs = dot_nt(g, v)
        grad_scores = (probability * (grad_probs - delta)).astype(jnp.bfloat16)
        part = dot_nn(grad_scores, k) * scale
        grad_query = part if grad_query is None else grad_query + part
    return grad_query, top, inverse, delta


def query_kernel(*refs, scale, n_short):
    q_ref, g_ref, qpos_ref, qss_ref, qsl_ref = refs[:5]
    shorts = [refs[5 + 4 * i : 9 + 4 * i] for i in range(n_short)]
    kl_ref, vl_ref, kpl_ref, ksl_ref = refs[5 + 4 * n_short : 9 + 4 * n_short]
    dq_ref, top_ref, inv_ref, delta_ref = refs[9 + 4 * n_short :]
    half = q_ref.shape[1] // 2
    for lo, hi, with_long in ((0, half, True), (half, 2 * half, False)):
        q = q_ref[0, lo:hi, :]
        g = g_ref[0, lo:hi, :]
        qpos = qpos_ref[0, lo:hi, :]
        qseg = qss_ref[0, lo:hi, :]
        parts = [
            (ks_ref[0], vs_ref[0], (kps_ref[0] <= qpos) & (kss_ref[0] == qseg))
            for ks_ref, vs_ref, kps_ref, kss_ref in shorts
        ]
        if with_long:
            parts.append(
                (kl_ref[0], vl_ref[0], (kpl_ref[0] <= qpos) & (ksl_ref[0] == qsl_ref[0, lo:hi, :]))
            )
        grad_query, top, inverse, delta = attend_rows(q, g, parts, scale)
        dq_ref[0, lo:hi, :] = grad_query.astype(dq_ref.dtype)
        top_ref[0, lo:hi, :] = top
        inv_ref[0, lo:hi, :] = inverse
        delta_ref[0, lo:hi, :] = delta


def key_rows(k, v, parts, scale):
    grad_key = None
    grad_value = None
    for q, g, live, stats in parts:
        scores = jnp.where(live, dot_nt(k, q) * scale, VERY_NEGATIVE)
        probability = jnp.where(live, jnp.exp(scores - stats[0:1, :]), 0.0) * stats[1:2, :]
        grad_probs = dot_nt(v, g)
        grad_scores = (probability * (grad_probs - stats[2:3, :])).astype(jnp.bfloat16)
        part_key = dot_nn(grad_scores, q) * scale
        part_value = dot_nn(probability.astype(jnp.bfloat16), g)
        grad_key = part_key if grad_key is None else grad_key + part_key
        grad_value = part_value if grad_value is None else grad_value + part_value
    return grad_key, grad_value


def key_kernel(
    k_ref, v_ref, qs_ref, gs_ref, ql_ref, gl_ref,
    kpos_ref, kss_ref, ksl_ref, qps_ref, qss_ref, sts_ref, qpl_ref, qsl_ref, stl_ref,
    dk_ref, dv_ref, *, scale,
):
    half = k_ref.shape[1] // 2
    qs = qs_ref[0]
    gs = gs_ref[0]
    sts = sts_ref[0]
    for lo, hi, with_long in ((0, half, True), (half, 2 * half, False)):
        k = k_ref[0, lo:hi, :]
        v = v_ref[0, lo:hi, :]
        kpos = kpos_ref[0, lo:hi, :]
        parts = [(qs, gs, (kpos <= qps_ref[0]) & (kss_ref[0, lo:hi, :] == qss_ref[0]), sts)]
        if with_long:
            parts.append(
                (
                    ql_ref[0],
                    gl_ref[0],
                    (kpos <= qpl_ref[0]) & (ksl_ref[0, lo:hi, :] == qsl_ref[0]),
                    stl_ref[0],
                )
            )
        grad_key, grad_value = key_rows(k, v, parts, scale)
        dk_ref[0, lo:hi, :] = grad_key.astype(dk_ref.dtype)
        dv_ref[0, lo:hi, :] = grad_value.astype(dv_ref.dtype)


def per_head(shape):
    return pl.BlockSpec((1,) + tuple(shape[1:]), lambda h: (h,) + (0,) * (len(shape) - 1))


def per_head_of(operand):
    if isinstance(operand, tuple):
        stacked, index = operand
        rest = (0,) * (stacked.ndim - 2)
        spec = pl.BlockSpec(
            (pl.Squeezed(), 1) + tuple(stacked.shape[2:]), lambda h: (index, h) + rest
        )
        return spec, stacked
    return per_head(operand.shape), operand


def run_per_head(kernel, inputs, out_shapes):
    heads = out_shapes[0].shape[0]
    specs, arrays = zip(*[per_head_of(x) for x in inputs])
    return pl.pallas_call(
        kernel,
        grid=(heads,),
        in_specs=list(specs),
        out_specs=[per_head(s.shape) for s in out_shapes],
        out_shape=out_shapes,
        compiler_params=pltpu.CompilerParams(dimension_semantics=("arbitrary",)),
    )(*arrays)


def column(x):
    return x[:, :, None]


def row(x):
    return x[:, None, :]


def shards(
    queries,
    key_vectors,
    value_vectors,
    grad_mixed,
    out_weight,
    head_phase,
    segments_short,
    segments_long,
):
    shard_index = lax.axis_index("seq")
    devices = lax.axis_size("seq")
    tok_dev = queries.shape[1]
    total = devices * tok_dev
    head_count = head_phase.shape[0]
    head_width = queries.shape[2] // head_count
    rows_short = tok_dev // 2
    rows_long = tok_dev // 4
    scale = 1.0 / math.sqrt(head_width)
    par_short = head_phase % 2
    par_long = head_phase // 2

    def split_rows(tensor):
        heads_major = jnp.transpose(tensor.reshape(tok_dev, head_count, head_width), (1, 0, 2))
        return take_rows(heads_major, par_short)

    def gathered(tensor):
        return lax.all_gather(tensor, "seq", axis=2, tiled=True)

    near_steps = [d for d in range(1, REACH_SHORT + 1) if d < devices]
    long_pos = row_positions(0, tok_dev, 4, head_phase, devices * rows_long)
    long_seg = segment_of(long_pos, segments_long)

    own_kv = jnp.stack([split_rows(key_vectors[0]), split_rows(value_vectors[0])])
    all_kv_long = gathered(take_rows(own_kv, par_long))
    near_kv = [own_kv] + [passed_along(own_kv, "seq", d) for d in near_steps]

    q_rows = split_rows(queries[0])
    core = shard_index % 2
    half_width = out_weight.shape[1] // 2
    own_half = lax.all_gather(
        lax.dynamic_slice_in_dim(out_weight, core * half_width, half_width, axis=1),
        "fsdp",
        axis=0,
        tiled=True,
    )
    other_half = lax.ppermute(own_half, "seq", [(i, i ^ 1) for i in range(devices)])
    grad_out = jnp.einsum(
        "td,rd->tr",
        lax.dynamic_slice_in_dim(grad_mixed[0], core * half_width, half_width, axis=1),
        own_half,
        preferred_element_type=jnp.float32,
    ) + jnp.einsum(
        "td,rd->tr",
        lax.dynamic_slice_in_dim(grad_mixed[0], (1 - core) * half_width, half_width, axis=1),
        other_half,
        preferred_element_type=jnp.float32,
    )
    grad_out = grad_out.astype(jnp.bfloat16)
    g_rows = split_rows(grad_out)
    own_qg = jnp.stack([q_rows, g_rows])
    all_qg_long = gathered(take_rows(own_qg, par_long))
    near_qg = [own_qg] + [passed_along(own_qg, "seq", -d) for d in near_steps]
    near_qg = jnp.concatenate(near_qg, axis=2)

    own_pos = row_positions(shard_index, tok_dev, 2, par_short, rows_short)
    own_seg_short = segment_of(own_pos, segments_short)
    own_is_long = (own_pos - head_phase[:, None]) % 4 == 0
    own_seg_long = jnp.where(own_is_long, segment_of(own_pos, segments_long), -3)

    short_keys = []
    for d, window in enumerate(near_kv):
        key_pos = row_positions(shard_index - d, tok_dev, 2, par_short, rows_short)
        key_seg = jnp.where(key_pos >= 0, segment_of(key_pos, segments_short), -1)
        short_keys += [(window, 0), (window, 1), row(key_pos), row(key_seg)]
    f32 = jnp.float32
    row_shape = jax.ShapeDtypeStruct((head_count, rows_short, head_width), jnp.bfloat16)
    stat_shape = jax.ShapeDtypeStruct((head_count, rows_short, 1), f32)
    grad_query, top, inverse, delta = run_per_head(
        functools.partial(query_kernel, scale=scale, n_short=len(near_kv)),
        [
            order_rows(q_rows, par_long),
            order_rows(g_rows, par_long),
            column(order_last(own_pos, par_long)),
            column(order_last(own_seg_short, par_long)),
            column(order_last(own_seg_long, par_long)),
        ]
        + short_keys
        + [(all_kv_long, 0), (all_kv_long, 1), row(long_pos), row(long_seg)],
        [row_shape, stat_shape, stat_shape, stat_shape],
    )
    grad_query = unorder_rows(grad_query, par_long)
    own_stats = unorder_last(
        jnp.stack([top[:, :, 0], inverse[:, :, 0], delta[:, :, 0]], axis=1), par_long
    )
    near_stats = [own_stats] + [passed_along(own_stats, "seq", -d) for d in near_steps]
    near_stats = jnp.concatenate(near_stats, axis=2)
    all_stats_long = lax.all_gather(
        take_stats(own_stats, par_long).reshape(3 * head_count, rows_long), "seq", axis=1, tiled=True
    ).reshape(head_count, 3, devices * rows_long)

    query_pos_short = window_positions(
        shard_index, list(range(len(near_steps) + 1)), tok_dev, 2, par_short, rows_short
    )
    query_seg_short = jnp.where(
        query_pos_short < total, segment_of(query_pos_short, segments_short), -2
    )
    ordered_kv = order_rows(own_kv, par_long)
    grad_key, grad_value = run_per_head(
        functools.partial(key_kernel, scale=scale),
        [
            (ordered_kv, 0),
            (ordered_kv, 1),
            (near_qg, 0),
            (near_qg, 1),
            (all_qg_long, 0),
            (all_qg_long, 1),
            column(order_last(own_pos, par_long)),
            column(order_last(own_seg_short, par_long)),
            column(order_last(own_seg_long, par_long)),
            row(query_pos_short),
            row(query_seg_short),
            near_stats,
            row(long_pos),
            row(long_seg),
            all_stats_long,
        ],
        [row_shape, row_shape],
    )
    grad_key = unorder_rows(grad_key, par_long)
    grad_value = unorder_rows(grad_value, par_long)

    def to_tokens(rows_here):
        tokens = put_rows(rows_here.astype(jnp.bfloat16), par_short)
        return jnp.transpose(tokens, (1, 0, 2)).reshape(1, tok_dev, head_count * head_width)

    return (to_tokens(grad_query), to_tokens(grad_key), to_tokens(grad_value))


def solution(mesh):
    placed = (
        P("fsdp", "seq", None),
        P("fsdp", "seq", None),
        P("fsdp", "seq", None),
        P("fsdp", "seq", None),
        P("fsdp", None),
        P(),
        P(),
        P(),
    )

    return jax.shard_map(
        shards,
        mesh=mesh,
        in_specs=placed,
        out_specs=(P("fsdp", "seq", None), P("fsdp", "seq", None), P("fsdp", "seq", None)),
        check_vma=False,
    )
```
